32 devices in a mesh: groups: 2 (over y), space: 4 (over z), sub: 2 (over x), ch: 2 (over core).
Axes of the slice: x: 2, y: 2, z: 4, core: 2. Of those that a mesh axis runs over, the one named last changes fastest.
Arguments:
- volumes: bfloat16 [4, 4, 32, 4, 256], P(('groups', 'sub'), None, None, 'space'), parts along dimension 0, may hold values from -6 to 6
- cotangent: bfloat16 [4, 4, 128, 2, 64], P(('groups', 'sub'), 'space', 'ch'), parts along dimension 0, may hold values from -6 to 6
- first_weight: bfloat16 [256, 128], P(None, 'ch'), may hold values from -0.375 to 0.375
- second_weight: bfloat16 [3456, 128], P(None, 'ch'), may hold values from -0.109375 to 0.109375
Outputs:
- block_out: bfloat16 [4, 4, 128, 2, 64], P(('groups', 'sub'), 'space', 'ch'), parts along dimension 0
- volume_grad: bfloat16 [4, 4, 32, 4, 256], P(('groups', 'sub'), None, 'ch', 'space'), parts along dimension 0
- first_grad: float32 [256, 256], P(('space', 'sub'), ('groups', 'ch')), parts along dimension 1
- second_grad: float32 [3456, 256], P(('space', 'sub'), ('groups', 'ch')), parts along dimension 1
The draws below stay inside these ranges and needn't reach their ends.
There are 2 independent parts, one for each index of `groups`. The reference program is written for one: setup_inputs(seed, part) draws one part's arguments, and reference() takes and returns one part's arrays. A program takes and returns all parts, laid end to end along the dimension named above; an argument that names none is the same for every part. Nothing has to cross between parts.
All inputs are finite; a program needn't handle non-finite values.
Results may differ from the reference program's by a relative error of at most 0.005.
Values may be sent and summed in bfloat16 or wider, within the bound.
No kernel may reach another device: no remote copies, remote signals or barrier semaphores. Data moves between devices by JAX's collectives and lax.ppermute only.
A program may use at most 64 MiB of HBM per device.

```python
import math
import jax
import jax.numpy as jnp
from jax import lax

C = 32
CO = 128
XY = 16
ROWS = 2
PER = 4
VZ = 4
HZ = 2
HXY = 8
VOX = 128


def level_of(own_key, extent, cuts, least, high):
    factor_of = 1.0
    for position, blocks in cuts:
        heights = jax.random.uniform(jax.random.fold_in(jax.random.fold_in(own_key, 6), position), (blocks,), jnp.float32, least / len(cuts), high / len(cuts))
        factor_of = factor_of * jnp.repeat(jnp.exp(heights), extent[position] // blocks).reshape((-1,) + (1,) * (len(extent) - 1 - position))
    return factor_of


def scatter_about(stream_key, dims, scale, most, shards=(), dtype=jnp.bfloat16):
    level = level_of(stream_key, dims, shards, -0.22, 0.18) if shards else 1.0
    entries = jax.random.normal(stream_key, dims, jnp.float32) * scale * level
    return jnp.minimum(jnp.maximum(entries, -most), most).astype(dtype)


def setup_inputs(seed: int = 0, part: int = 0) -> dict:
    splits = jax.random.split(jax.random.key(seed), 5)
    part_keys = jax.random.split(jax.random.fold_in(splits[4], part), 5)
    return {
        "volumes": scatter_about(part_keys[0], (ROWS, PER, C, VZ, XY * XY), 1.0, 6.0, ((0, 2), (3, 4))),
        "cotangent": scatter_about(part_keys[1], (ROWS, PER, CO, HZ, HXY * HXY), 1.0, 6.0, ((0, 2), (1, 4), (2, 2))),
        "first_weight": scatter_about(splits[2], (8 * C, CO), (8 * C) ** -0.5, 0.375, ((1, 2),)),
        "second_weight": scatter_about(splits[3], (27 * CO, CO), (27 * CO) ** -0.5, 0.109375, ((1, 2),)),
    }


def to_depth(sample, side):
    chans, depth = (sample.shape[0], sample.shape[1])
    blocks = sample.reshape(chans, depth // 2, 2, side // 2, 2, side // 2, 2)
    blocks = blocks.transpose(2, 4, 6, 0, 1, 3, 5)
    return blocks.reshape(8 * chans, depth // 2 * (side // 2) * (side // 2))

def from_depth(cols, chans, depth, side):
    blocks = cols.reshape(2, 2, 2, chans, depth // 2, side // 2, side // 2)
    blocks = blocks.transpose(3, 4, 0, 5, 1, 6, 2)
    return blocks.reshape(chans, depth, side * side)

def plane_stack(padded, plane, depth, side, flip):
    chans = padded.shape[0]
    windows = []
    for inner in range(9):
        b, c = (inner // 3, inner % 3)
        if flip:
            window = padded[:, 2 - plane:2 - plane + depth, 2 - b:2 - b + side, 2 - c:2 - c + side]
        else:
            window = padded[:, plane:plane + depth, b:b + side, c:c + side]
        windows.append(window.reshape(chans, depth * side * side))
    return jnp.concatenate(windows, axis=0)

def conv_forward(hidden, weight):
    chans, depth, side = (hidden.shape[0], hidden.shape[1], hidden.shape[2])
    padded = jnp.pad(hidden, ((0, 0), (1, 1), (1, 1), (1, 1)))
    total = jnp.zeros((weight.shape[1], depth * side * side), jnp.float32)
    for plane in range(3):
        stacked = plane_stack(padded, plane, depth, side, False)
        piece = weight[plane * 9 * chans:(plane + 1) * 9 * chans]
        total = total + lax.dot_general(piece, stacked, (((0,), (0,)), ((), ())), preferred_element_type=jnp.float32)
    return total

def conv_weight_grad(hidden, cot):
    chans, depth, side = (hidden.shape[0], hidden.shape[1], hidden.shape[2])
    padded = jnp.pad(hidden, ((0, 0), (1, 1), (1, 1), (1, 1)))
    pieces = []
    for plane in range(3):
        stacked = plane_stack(padded, plane, depth, side, False)
        pieces.append(lax.dot_general(stacked, cot, (((1,), (1,)), ((), ())), preferred_element_type=jnp.float32))
    return jnp.concatenate(pieces, axis=0)

def conv_back(cot, weight_rows):
    chans, depth, side = (cot.shape[0], cot.shape[1], cot.shape[2])
    padded = jnp.pad(cot, ((0, 0), (1, 1), (1, 1), (1, 1)))
    total = jnp.zeros((weight_rows.shape[1], depth * side * side), jnp.float32)
    for plane in range(3):
        stacked = plane_stack(padded, plane, depth, side, True)
        group = weight_rows[plane * 9:(plane + 1) * 9]
        lhs = group.transpose(1, 0, 2).reshape(group.shape[1], 9 * group.shape[2])
        total = total + jnp.dot(lhs, stacked, preferred_element_type=jnp.float32)
    return total

def silu_slope(pre):
    sig = jax.nn.sigmoid(pre)
    return sig * (1.0 + pre * (1.0 - sig))

def reference(volumes, cotangent, first_weight, second_weight):
    chans = volumes.shape[2]
    width = second_weight.shape[1]
    count = ROWS * PER
    flat_vol = volumes.reshape(count, chans, VZ, XY * XY)
    flat_cot = cotangent.reshape(count, width, HZ, HXY, HXY)
    weight_rows = second_weight.reshape(27, width, width)
    factor = 1.0 / math.sqrt(count * VOX)

    def one(carry, item):
        sample, cot = item
        cols = to_depth(sample, XY)
        pre = lax.dot_general(first_weight, cols, (((0,), (0,)), ((), ())), preferred_element_type=jnp.float32)
        hidden = jax.nn.silu(pre).astype(jnp.bfloat16)
        grid = hidden.reshape(width, HZ, HXY, HXY)
        out = conv_forward(grid, second_weight).astype(jnp.bfloat16)
        grad_two = conv_weight_grad(grid, cot.reshape(width, VOX))
        hidden_grad = conv_back(cot, weight_rows)
        pre_grad = (hidden_grad * silu_slope(pre)).astype(jnp.bfloat16)
        grad_one = lax.dot_general(cols, pre_grad, (((1,), (1,)), ((), ())), preferred_element_type=jnp.float32)
        grad_cols = jnp.dot(first_weight, pre_grad, preferred_element_type=jnp.float32)
        grad_vol = from_depth(grad_cols, chans, VZ, XY).astype(jnp.bfloat16)
        return ((carry[0] + grad_one, carry[1] + grad_two), (out, grad_vol))
    init = (jnp.zeros((8 * chans, width), jnp.float32), jnp.zeros((27 * width, width), jnp.float32))
    sums, stacked = lax.scan(one, init, (flat_vol, flat_cot))
    outs, grads = stacked
    block_out = outs.reshape(ROWS, PER, width, HZ, HXY * HXY)
    volume_grad = grads.reshape(ROWS, PER, chans, VZ, XY * XY)
    return (block_out, volume_grad, sums[0] * factor, sums[1] * factor)
```

```python
import math

import jax
import jax.numpy as jnp
from jax import lax
from jax.sharding import PartitionSpec as P

XY = 16


def to_depth(sample, side):
    chans, depth = (sample.shape[0], sample.shape[1])
    blocks = sample.reshape(chans, depth // 2, 2, side // 2, 2, side // 2, 2)
    blocks = blocks.transpose(2, 4, 6, 0, 1, 3, 5)
    return blocks.reshape(8 * chans, depth // 2 * (side // 2) * (side // 2))


def from_depth(cols, chans, depth, side):
    blocks = cols.reshape(2, 2, 2, chans, depth // 2, side // 2, side // 2)
    blocks = blocks.transpose(3, 4, 0, 5, 1, 6, 2)
    return blocks.reshape(chans, depth, side * side)


def plane_stack(padded, plane, depth, side, flip):
    chans = padded.shape[0]
    windows = []
    for inner in range(9):
        b, c = (inner // 3, inner % 3)
        if flip:
            window = padded[
                :, 2 - plane : 2 - plane + depth, 2 - b : 2 - b + side, 2 - c : 2 - c + side
            ]
        else:
            window = padded[:, plane : plane + depth, b : b + side, c : c + side]
        windows.append(window.reshape(chans, depth * side * side))
    return jnp.concatenate(windows, axis=0)


def conv_forward(hidden, weight):
    chans, depth, side = (hidden.shape[0], hidden.shape[1], hidden.shape[2])
    padded = jnp.pad(hidden, ((0, 0), (1, 1), (1, 1), (1, 1)))
    total = jnp.zeros((weight.shape[1], depth * side * side), jnp.float32)
    for plane in range(3):
        stacked = plane_stack(padded, plane, depth, side, False)
        piece = weight[plane * 9 * chans : (plane + 1) * 9 * chans]
        total = total + lax.dot_general(
            piece, stacked, (((0,), (0,)), ((), ())), preferred_element_type=jnp.float32
        )
    return total


def conv_weight_grad(hidden, cot):
    chans, depth, side = (hidden.shape[0], hidden.shape[1], hidden.shape[2])
    padded = jnp.pad(hidden, ((0, 0), (1, 1), (1, 1), (1, 1)))
    pieces = []
    for plane in range(3):
        stacked = plane_stack(padded, plane, depth, side, False)
        pieces.append(
            lax.dot_general(
                stacked, cot, (((1,), (1,)), ((), ())), preferred_element_type=jnp.float32
            )
        )
    return jnp.concatenate(pieces, axis=0)


def conv_back(cot, weight_rows):
    chans, depth, side = (cot.shape[0], cot.shape[1], cot.shape[2])
    padded = jnp.pad(cot, ((0, 0), (1, 1), (1, 1), (1, 1)))
    total = jnp.zeros((weight_rows.shape[1], depth * side * side), jnp.float32)
    for plane in range(3):
        stacked = plane_stack(padded, plane, depth, side, True)
        group = weight_rows[plane * 9 : (plane + 1) * 9]
        lhs = group.transpose(1, 0, 2).reshape(group.shape[1], 9 * group.shape[2])
        total = total + jnp.dot(lhs, stacked, preferred_element_type=jnp.float32)
    return total


def halving_scatter(x, names):
    sizes = [lax.axis_size(n) for n in names]
    labels = []
    for name, size in zip(names, sizes):
        bits = size.bit_length() - 1
        labels += [(name, j) for j in reversed(range(bits))]
    rows = x.shape[0] // math.prod(sizes)
    x = x.reshape((2,) * len(labels) + (rows,) + x.shape[1:])
    for name, size in reversed(list(zip(names, sizes))):
        for j in range(size.bit_length() - 1):
            pos = labels.index((name, j))
            bit = (lax.axis_index(name) >> j) & 1
            mine = lax.dynamic_index_in_dim(x, bit, axis=pos, keepdims=False)
            other = lax.dynamic_index_in_dim(x, 1 - bit, axis=pos, keepdims=False)
            perm = [(i, i ^ (1 << j)) for i in range(size)]
            x = mine + lax.ppermute(other, name, perm)
            labels.pop(pos)
    return x


def silu_slope(pre):
    sig = jax.nn.sigmoid(pre)
    return sig * (1.0 + pre * (1.0 - sig))


def body(volumes, cotangent, first_weight, second_weight):
    chans = volumes.shape[2]
    half_c = chans // lax.axis_size("ch")
    pair_index = lax.axis_index("ch")
    half_o = first_weight.shape[1]
    sample = lax.all_to_all(volumes, "space", split_axis=1, concat_axis=3, tiled=True)
    depth = sample.shape[3]
    sample = sample.reshape(chans, depth, XY * XY)
    half_z, half_s = (depth // 2, XY // 2)
    voxels = half_z * half_s * half_s
    cols = to_depth(sample, XY)
    pre = lax.dot_general(
        first_weight, cols, (((0,), (0,)), ((), ())), preferred_element_type=jnp.float32
    )
    hidden = jax.nn.silu(pre).astype(jnp.bfloat16)
    grid = lax.all_gather(hidden.reshape(half_o, half_z, half_s, half_s), "ch", axis=0, tiled=True)
    width = grid.shape[0]
    out = conv_forward(grid, second_weight)
    block_out = out.astype(jnp.bfloat16).reshape(1, 1, half_o, half_z, half_s * half_s)
    cot = cotangent.reshape(half_o, voxels)
    factor = 1.0 / math.sqrt(lax.axis_size("space") * lax.axis_size("sub") * voxels)
    grad_second = conv_weight_grad(grid, cot) * factor
    cot_grid = cot.reshape(half_o, half_z, half_s, half_s)
    local_rows = second_weight.reshape(27, width, half_o)
    hidden_grad = halving_scatter(conv_back(cot_grid, local_rows), ("ch",))
    pre_grad = (hidden_grad * silu_slope(pre)).astype(jnp.bfloat16)
    grad_first = (
        lax.dot_general(
            cols, pre_grad, (((1,), (1,)), ((), ())), preferred_element_type=jnp.float32
        )
        * factor
    )
    all_pre_grad, all_first = (
        lax.all_gather(pre_grad, "ch", axis=0, tiled=True),
        lax.all_gather(first_weight, "ch", axis=1, tiled=True),
    )
    first_rows = lax.dynamic_slice_in_dim(
        all_first.reshape(8, chans, width), pair_index * half_c, half_c, 1
    )
    grad_cols = jnp.dot(
        first_rows.reshape(8 * half_c, width), all_pre_grad, preferred_element_type=jnp.float32
    )
    grad_sample = from_depth(grad_cols, half_c, depth, XY).astype(jnp.bfloat16)
    volume_grad = lax.all_to_all(
        grad_sample.reshape(1, 1, half_c, depth, XY * XY),
        "space",
        split_axis=3,
        concat_axis=1,
        tiled=True,
    )
    first_grad, second_grad = (
        halving_scatter(grad_first, ("space", "sub")),
        halving_scatter(grad_second, ("space", "sub")),
    )
    return (block_out, volume_grad, first_grad, second_grad)


def solution(mesh):
    return jax.shard_map(
        body,
        mesh=mesh,
        in_specs=(
            P(("groups", "sub"), None, None, "space", None),
            P(("groups", "sub"), "space", "ch", None, None),
            P(None, "ch"),
            P(None, "ch"),
        ),
        out_specs=(
            P(("groups", "sub"), "space", "ch", None, None),
            P(("groups", "sub"), None, "ch", "space", None),
            P(("space", "sub"), ("groups", "ch")),
            P(("space", "sub"), ("groups", "ch")),
        ),
        check_vma=False,
    )
```

```python
import math

import jax
import jax.numpy as jnp
from jax import lax
from jax.sharding import PartitionSpec as P

XY = 16


def to_depth(sample, side):
    chans, depth = (sample.shape[0], sample.shape[1])
    blocks = sample.reshape(chans, depth // 2, 2, side // 2, 2, side // 2, 2)
    blocks = blocks.transpose(2, 4, 6, 0, 1, 3, 5)
    return blocks.reshape(8 * chans, depth // 2 * (side // 2) * (side // 2))


def from_depth(cols, chans, depth, side):
    blocks = cols.reshape(2, 2, 2, chans, depth // 2, side // 2, side // 2)
    blocks = blocks.transpose(3, 4, 0, 5, 1, 6, 2)
    return blocks.reshape(chans, depth, side * side)


def plane_stack(padded, plane, depth, side, flip):
    chans = padded.shape[0]
    windows = []
    for inner in range(9):
        b, c = (inner // 3, inner % 3)
        if flip:
            window = padded[
                :, 2 - plane : 2 - plane + depth, 2 - b : 2 - b + side, 2 - c : 2 - c + side
            ]
        else:
            window = padded[:, plane : plane + depth, b : b + side, c : c + side]
        windows.append(window.reshape(chans, depth * side * side))
    return jnp.concatenate(windows, axis=0)


def conv_forward(hidden, weight):
    chans, depth, side = (hidden.shape[0], hidden.shape[1], hidden.shape[2])
    padded = jnp.pad(hidden, ((0, 0), (1, 1), (1, 1), (1, 1)))
    total = jnp.zeros((weight.shape[1], depth * side * side), jnp.float32)
    for plane in range(3):
        stacked = plane_stack(padded, plane, depth, side, False)
        piece = weight[plane * 9 * chans : (plane + 1) * 9 * chans]
        total = total + lax.dot_general(
            piece, stacked, (((0,), (0,)), ((), ())), preferred_element_type=jnp.float32
        )
    return total


def conv_weight_grad(hidden, cot):
    chans, depth, side = (hidden.shape[0], hidden.shape[1], hidden.shape[2])
    padded = jnp.pad(hidden, ((0, 0), (1, 1), (1, 1), (1, 1)))
    pieces = []
    for plane in range(3):
        stacked = plane_stack(padded, plane, depth, side, False)
        pieces.append(
            lax.dot_general(
                stacked, cot, (((1,), (1,)), ((), ())), preferred_element_type=jnp.float32
            )
        )
    return jnp.concatenate(pieces, axis=0)


def conv_back(cot, weight_rows):
    chans, depth, side = (cot.shape[0], cot.shape[1], cot.shape[2])
    padded = jnp.pad(cot, ((0, 0), (1, 1), (1, 1), (1, 1)))
    total = jnp.zeros((weight_rows.shape[1], depth * side * side), jnp.float32)
    for plane in range(3):
        stacked = plane_stack(padded, plane, depth, side, True)
        group = weight_rows[plane * 9 : (plane + 1) * 9]
        lhs = group.transpose(1, 0, 2).reshape(group.shape[1], 9 * group.shape[2])
        total = total + jnp.dot(lhs, stacked, preferred_element_type=jnp.float32)
    return total


def halving_scatter(x, names):
    sizes = [lax.axis_size(n) for n in names]
    labels = []
    for name, size in zip(names, sizes):
        bits = size.bit_length() - 1
        labels += [(name, j) for j in reversed(range(bits))]
    rows = x.shape[0] // math.prod(sizes)
    x = x.reshape((2,) * len(labels) + (rows,) + x.shape[1:])
    for name, size in reversed(list(zip(names, sizes))):
        for j in range(size.bit_length() - 1):
            pos = labels.index((name, j))
            bit = (lax.axis_index(name) >> j) & 1
            mine = lax.dynamic_index_in_dim(x, bit, axis=pos, keepdims=False)
            other = lax.dynamic_index_in_dim(x, 1 - bit, axis=pos, keepdims=False)
            perm = [(i, i ^ (1 << j)) for i in range(size)]
            x = mine + lax.ppermute(other, name, perm)
            labels.pop(pos)
    return x


def doubling_gather(x, names):
    for name in reversed(names):
        size = lax.axis_size(name)
        for j in range(size.bit_length() - 1):
            perm = [(i, i ^ (1 << j)) for i in range(size)]
            x = jnp.concatenate([x, lax.ppermute(x, name, perm)], axis=0)
    return x


def second_grad_rows(hidden_all, cot_all, names, total_rows):
    count, chans, depth, side = hidden_all.shape[0], hidden_all.shape[1], hidden_all.shape[2], hidden_all.shape[3]
    shards = math.prod(lax.axis_size(n) for n in names)
    rows = total_rows // shards
    index = 0
    for name in names:
        index = index * lax.axis_size(name) + lax.axis_index(name)
    first = index * rows
    tap0 = first // chans
    taps = min(27, (rows + 2 * chans - 2) // chans)
    padded = jnp.pad(hidden_all, ((0, 0), (0, 0), (1, 1), (1, 1), (1, 1)))
    pieces = []
    for slot in range(taps):
        tap = jnp.minimum(tap0 + slot, 26)
        window = lax.dynamic_slice(
            padded, (0, 0, tap // 9, (tap // 3) % 3, tap % 3), (count, chans, depth, side, side)
        ).reshape(count, chans, depth * side * side)
        pieces.append(
            lax.dot_general(
                window, cot_all, (((0, 2), (0, 2)), ((), ())), preferred_element_type=jnp.float32
            )
        )
    stacked = jnp.concatenate(pieces, axis=0)
    return lax.dynamic_slice_in_dim(stacked, first - tap0 * chans, rows, 0)


def silu_slope(pre):
    sig = jax.nn.sigmoid(pre)
    return sig * (1.0 + pre * (1.0 - sig))


def body(volumes, cotangent, first_weight, second_weight):
    chans = volumes.shape[2]
    half_c = chans // lax.axis_size("ch")
    pair_index = lax.axis_index("ch")
    half_o = first_weight.shape[1]
    sample = lax.all_to_all(volumes, "space", split_axis=1, concat_axis=3, tiled=True)
    depth = sample.shape[3]
    sample = sample.reshape(chans, depth, XY * XY)
    half_z, half_s = (depth // 2, XY // 2)
    voxels = half_z * half_s * half_s
    cols = to_depth(sample, XY)
    pre = lax.dot_general(
        first_weight, cols, (((0,), (0,)), ((), ())), preferred_element_type=jnp.float32
    )
    hidden = jax.nn.silu(pre).astype(jnp.bfloat16)
    grid = lax.all_gather(hidden.reshape(half_o, half_z, half_s, half_s), "ch", axis=0, tiled=True)
    width = grid.shape[0]
    out = conv_forward(grid, second_weight)
    block_out = out.astype(jnp.bfloat16).reshape(1, 1, half_o, half_z, half_s * half_s)
    cot = cotangent.reshape(half_o, voxels)
    factor = 1.0 / math.sqrt(lax.axis_size("space") * lax.axis_size("sub") * voxels)
    shards = lax.axis_size("space") * lax.axis_size("sub")
    gather_second = shards * (width + half_o) * voxels * 2 <= 1 << 22
    if gather_second:
        both = doubling_gather(
            jnp.concatenate([grid.reshape(width, voxels), cot], axis=0)[None], ("space", "sub")
        )
        grad_second = (
            second_grad_rows(
                both[:, :width].reshape(both.shape[0], width, half_z, half_s, half_s),
                both[:, width:],
                ("space", "sub"),
                second_weight.shape[0],
            )
            * factor
        )
    else:
        grad_second = conv_weight_grad(grid, cot) * factor
    cot_grid = cot.reshape(half_o, half_z, half_s, half_s)
    local_rows = second_weight.reshape(27, width, half_o)
    hidden_grad = halving_scatter(conv_back(cot_grid, local_rows), ("ch",))
    pre_grad = (hidden_grad * silu_slope(pre)).astype(jnp.bfloat16)
    grad_first = (
        lax.dot_general(
            cols, pre_grad, (((1,), (1,)), ((), ())), preferred_element_type=jnp.float32
        )
        * factor
    )
    all_pre_grad, all_first = (
        lax.all_gather(pre_grad, "ch", axis=0, tiled=True),
        lax.all_gather(first_weight, "ch", axis=1, tiled=True),
    )
    first_rows = lax.dynamic_slice_in_dim(
        all_first.reshape(8, chans, width), pair_index * half_c, half_c, 1
    )
    grad_cols = jnp.dot(
        first_rows.reshape(8 * half_c, width), all_pre_grad, preferred_element_type=jnp.float32
    )
    grad_sample = from_depth(grad_cols, half_c, depth, XY).astype(jnp.bfloat16)
    volume_grad = lax.all_to_all(
        grad_sample.reshape(1, 1, half_c, depth, XY * XY),
        "space",
        split_axis=3,
        concat_axis=1,
        tiled=True,
    )
    first_grad, second_grad = (
        halving_scatter(grad_first, ("space", "sub")),
        grad_second if gather_second else halving_scatter(grad_second, ("space", "sub")),
    )
    return (block_out, volume_grad, first_grad, second_grad)


def solution(mesh):
    return jax.shard_map(
        body,
        mesh=mesh,
        in_specs=(
            P(("groups", "sub"), None, None, "space", None),
            P(("groups", "sub"), "space", "ch", None, None),
            P(None, "ch"),
            P(None, "ch"),
        ),
        out_specs=(
            P(("groups", "sub"), "space", "ch", None, None),
            P(("groups", "sub"), None, "ch", "space", None),
            P(("space", "sub"), ("groups", "ch")),
            P(("space", "sub"), ("groups", "ch")),
        ),
        check_vma=False,
    )
```

```python
import math

import jax
import jax.numpy as jnp
from jax import lax
from jax.sharding import PartitionSpec as P


XY = 16


def to_depth(sample, side):
    chans, depth = (sample.shape[0], sample.shape[1])
    blocks = sample.reshape(chans, depth // 2, 2, side // 2, 2, side // 2, 2)
    blocks = blocks.transpose(2, 4, 6, 0, 1, 3, 5)
    return blocks.reshape(8 * chans, depth // 2 * (side // 2) * (side // 2))


def from_depth(cols, chans, depth, side):
    blocks = cols.reshape(2, 2, 2, chans, depth // 2, side // 2, side // 2)
    blocks = blocks.transpose(3, 4, 0, 5, 1, 6, 2)
    return blocks.reshape(chans, depth, side * side)


def plane_stack(padded, plane, depth, side, flip):
    chans = padded.shape[0]
    windows = []
    for inner in range(9):
        b, c = (inner // 3, inner % 3)
        if flip:
            window = padded[
                :, 2 - plane : 2 - plane + depth, 2 - b : 2 - b + side, 2 - c : 2 - c + side
            ]
        else:
            window = padded[:, plane : plane + depth, b : b + side, c : c + side]
        windows.append(window.reshape(chans, depth * side * side))
    return jnp.concatenate(windows, axis=0)


def conv_forward(hidden, weight):
    chans, depth, side = (hidden.shape[0], hidden.shape[1], hidden.shape[2])
    padded = jnp.pad(hidden, ((0, 0), (1, 1), (1, 1), (1, 1)))
    total = jnp.zeros((weight.shape[1], depth * side * side), jnp.float32)
    for plane in range(3):
        stacked = plane_stack(padded, plane, depth, side, False)
        piece = weight[plane * 9 * chans : (plane + 1) * 9 * chans]
        total = total + lax.dot_general(
            piece, stacked, (((0,), (0,)), ((), ())), preferred_element_type=jnp.float32
        )
    return total


def conv_weight_grad(hidden, cot):
    depth, side = (hidden.shape[1], hidden.shape[2])
    padded = jnp.pad(hidden, ((0, 0), (1, 1), (1, 1), (1, 1)))
    pieces = []
    for plane in range(3):
        stacked = plane_stack(padded, plane, depth, side, False)
        pieces.append(
            lax.dot_general(
                stacked, cot, (((1,), (1,)), ((), ())), preferred_element_type=jnp.float32
            )
        )
    return jnp.concatenate(pieces, axis=0)


def conv_back(cot, weight_rows):
    depth, side = (cot.shape[1], cot.shape[2])
    padded = jnp.pad(cot, ((0, 0), (1, 1), (1, 1), (1, 1)))
    total = jnp.zeros((weight_rows.shape[1], depth * side * side), jnp.float32)
    for plane in range(3):
        stacked = plane_stack(padded, plane, depth, side, True)
        group = weight_rows[plane * 9 : (plane + 1) * 9]
        lhs = group.transpose(1, 0, 2).reshape(group.shape[1], 9 * group.shape[2])
        total = total + jnp.dot(lhs, stacked, preferred_element_type=jnp.float32)
    return total


def halving_scatter(x, names):
    sizes = [lax.axis_size(n) for n in names]
    labels = []
    for name, size in zip(names, sizes):
        bits = size.bit_length() - 1
        labels += [(name, j) for j in reversed(range(bits))]
    rows = x.shape[0] // math.prod(sizes)
    x = x.reshape((2,) * len(labels) + (rows,) + x.shape[1:])
    for name, size in reversed(list(zip(names, sizes))):
        for j in range(size.bit_length() - 1):
            pos = labels.index((name, j))
            bit = (lax.axis_index(name) >> j) & 1
            mine = lax.dynamic_index_in_dim(x, bit, axis=pos, keepdims=False)
            other = lax.dynamic_index_in_dim(x, 1 - bit, axis=pos, keepdims=False)
            perm = [(i, i ^ (1 << j)) for i in range(size)]
            x = mine + lax.ppermute(other, name, perm)
            labels.pop(pos)
    return x


def second_grad_rows(hidden_all, cot_all, names, total_rows):
    count, chans, depth, side = hidden_all.shape[0], hidden_all.shape[1], hidden_all.shape[2], hidden_all.shape[3]
    shards = math.prod(lax.axis_size(n) for n in names)
    rows = total_rows // shards
    index = 0
    for name in names:
        index = index * lax.axis_size(name) + lax.axis_index(name)
    first = index * rows
    tap0 = first // chans
    taps = min(27, (rows + 2 * chans - 2) // chans)
    padded = jnp.pad(hidden_all, ((0, 0), (0, 0), (1, 1), (1, 1), (1, 1)))
    pieces = []
    for slot in range(taps):
        tap = jnp.minimum(tap0 + slot, 26)
        window = lax.dynamic_slice(
            padded, (0, 0, tap // 9, (tap // 3) % 3, tap % 3), (count, chans, depth, side, side)
        ).reshape(count, chans, depth * side * side)
        pieces.append(
            lax.dot_general(
                window, cot_all, (((0, 2), (0, 2)), ((), ())), preferred_element_type=jnp.float32
            )
        )
    stacked = jnp.concatenate(pieces, axis=0)
    return lax.dynamic_slice_in_dim(stacked, first - tap0 * chans, rows, 0)


def group_index(names):
    index = 0
    for name in names:
        index = index * lax.axis_size(name) + lax.axis_index(name)
    return index


def direct_gather(x, names):
    count = math.prod(lax.axis_size(n) for n in names)
    pieces = [x]
    for d in range(1, count):
        pieces.append(lax.ppermute(x, names, [(k, k ^ d) for k in range(count)]))
    return jnp.concatenate(pieces, axis=0)


def direct_scatter(x, names):
    count = math.prod(lax.axis_size(n) for n in names)
    if count > 8:
        return halving_scatter(x, names)
    index = group_index(names)
    blocks = x.reshape((count, x.shape[0] // count) + x.shape[1:])
    total = lax.dynamic_index_in_dim(blocks, index, keepdims=False)
    for d in range(1, count):
        piece = lax.dynamic_index_in_dim(blocks, index ^ d, keepdims=False)
        total = total + lax.ppermute(piece, names, [(k, k ^ d) for k in range(count)])
    return total


def silu_slope(pre):
    sig = jax.nn.sigmoid(pre)
    return sig * (1.0 + pre * (1.0 - sig))


def block(volumes, cotangent, first_weight, second_weight):
    chans = volumes.shape[2]
    half_c = chans // lax.axis_size("ch")
    pair_index = lax.axis_index("ch")
    half_o = first_weight.shape[1]
    sample = lax.all_to_all(volumes, "space", split_axis=1, concat_axis=3, tiled=True)
    depth = sample.shape[3]
    sample = sample.reshape(chans, depth, XY * XY)
    half_z, half_s = (depth // 2, XY // 2)
    voxels = half_z * half_s * half_s
    cols = to_depth(sample, XY)
    pre = lax.dot_general(
        first_weight, cols, (((0,), (0,)), ((), ())), preferred_element_type=jnp.float32
    )
    hidden = jax.nn.silu(pre).astype(jnp.bfloat16)
    grid = lax.all_gather(hidden.reshape(half_o, half_z, half_s, half_s), "ch", axis=0, tiled=True)
    width = grid.shape[0]
    out = conv_forward(grid, second_weight)
    block_out = out.astype(jnp.bfloat16).reshape(1, 1, half_o, half_z, half_s * half_s)
    cot = cotangent.reshape(half_o, voxels)
    factor = 1.0 / math.sqrt(lax.axis_size("space") * lax.axis_size("sub") * voxels)
    shards = lax.axis_size("space") * lax.axis_size("sub")
    gather_second = shards * (width + half_o) * voxels * 2 <= 1 << 22
    if gather_second:
        both = direct_gather(
            jnp.concatenate([grid.reshape(width, voxels), cot], axis=0)[None], ("space", "sub")
        )
        grad_second = (
            second_grad_rows(
                both[:, :width].reshape(both.shape[0], width, half_z, half_s, half_s),
                both[:, width:],
                ("space", "sub"),
                second_weight.shape[0],
            )
            * factor
        )
    else:
        grad_second = conv_weight_grad(grid, cot) * factor
    cot_grid = cot.reshape(half_o, half_z, half_s, half_s)
    local_rows = second_weight.reshape(27, width, half_o)
    hidden_grad = halving_scatter(conv_back(cot_grid, local_rows), ("ch",))
    pre_grad = (hidden_grad * silu_slope(pre)).astype(jnp.bfloat16)
    grad_first = (
        lax.dot_general(
            cols, pre_grad, (((1,), (1,)), ((), ())), preferred_element_type=jnp.float32
        )
        * factor
    )
    all_pre_grad = lax.all_gather(pre_grad, "ch", axis=0, tiled=True)
    all_first = lax.all_gather(first_weight, "ch", axis=1, tiled=True)
    first_rows = lax.dynamic_slice_in_dim(
        all_first.reshape(8, chans, width), pair_index * half_c, half_c, 1
    )
    grad_cols = jnp.dot(
        first_rows.reshape(8 * half_c, width), all_pre_grad, preferred_element_type=jnp.float32
    )
    grad_sample = from_depth(grad_cols, half_c, depth, XY).astype(jnp.bfloat16)
    volume_grad = lax.all_to_all(
        grad_sample.reshape(1, 1, half_c, depth, XY * XY),
        "space",
        split_axis=3,
        concat_axis=1,
        tiled=True,
    )
    first_grad = direct_scatter(grad_first, ("space", "sub"))
    second_grad = (
        grad_second if gather_second else halving_scatter(grad_second, ("space", "sub"))
    )
    return (block_out, volume_grad, first_grad, second_grad)


def solution(mesh):
    return step_of(mesh)


def step_of(mesh):
    return jax.shard_map(
        block,
        mesh=mesh,
        in_specs=(
            P(("groups", "sub"), None, None, "space", None),
            P(("groups", "sub"), "space", "ch", None, None),
            P(None, "ch"),
            P(None, "ch"),
        ),
        out_specs=(
            P(("groups", "sub"), "space", "ch", None, None),
            P(("groups", "sub"), None, "ch", "space", None),
            P(("space", "sub"), ("groups", "ch")),
            P(("space", "sub"), ("groups", "ch")),
        ),
        check_vma=False,
    )
```

```python
import math

import jax
import jax.numpy as jnp
from jax import lax
from jax.sharding import PartitionSpec as P


XY = 16


def to_depth(sample, side):
    chans, depth = (sample.shape[0], sample.shape[1])
    blocks = sample.reshape(chans, depth // 2, 2, side // 2, 2, side // 2, 2)
    blocks = blocks.transpose(2, 4, 6, 0, 1, 3, 5)
    return blocks.reshape(8 * chans, depth // 2 * (side // 2) * (side // 2))


def from_depth(cols, chans, depth, side):
    blocks = cols.reshape(2, 2, 2, chans, depth // 2, side // 2, side // 2)
    blocks = blocks.transpose(3, 4, 0, 5, 1, 6, 2)
    return blocks.reshape(chans, depth, side * side)


def plane_stack(padded, plane, depth, side, flip):
    chans = padded.shape[0]
    windows = []
    for inner in range(9):
        b, c = (inner // 3, inner % 3)
        if flip:
            window = padded[
                :, 2 - plane : 2 - plane + depth, 2 - b : 2 - b + side, 2 - c : 2 - c + side
            ]
        else:
            window = padded[:, plane : plane + depth, b : b + side, c : c + side]
        windows.append(window.reshape(chans, depth * side * side))
    return jnp.concatenate(windows, axis=0)


def conv_forward(hidden, weight):
    chans, depth, side = (hidden.shape[0], hidden.shape[1], hidden.shape[2])
    padded = jnp.pad(hidden, ((0, 0), (1, 1), (1, 1), (1, 1)))
    total = jnp.zeros((weight.shape[1], depth * side * side), jnp.float32)
    for plane in range(3):
        stacked = plane_stack(padded, plane, depth, side, False)
        piece = weight[plane * 9 * chans : (plane + 1) * 9 * chans]
        total = total + lax.dot_general(
            piece, stacked, (((0,), (0,)), ((), ())), preferred_element_type=jnp.float32
        )
    return total


def conv_weight_grad(hidden, cot):
    depth, side = (hidden.shape[1], hidden.shape[2])
    padded = jnp.pad(hidden, ((0, 0), (1, 1), (1, 1), (1, 1)))
    pieces = []
    for plane in range(3):
        stacked = plane_stack(padded, plane, depth, side, False)
        pieces.append(
            lax.dot_general(
                stacked, cot, (((1,), (1,)), ((), ())), preferred_element_type=jnp.float32
            )
        )
    return jnp.concatenate(pieces, axis=0)


def conv_back(cot, weight_rows):
    depth, side = (cot.shape[1], cot.shape[2])
    padded = jnp.pad(cot, ((0, 0), (1, 1), (1, 1), (1, 1)))
    total = jnp.zeros((weight_rows.shape[1], depth * side * side), jnp.float32)
    for plane in range(3):
        stacked = plane_stack(padded, plane, depth, side, True)
        group = weight_rows[plane * 9 : (plane + 1) * 9]
        lhs = group.transpose(1, 0, 2).reshape(group.shape[1], 9 * group.shape[2])
        total = total + jnp.dot(lhs, stacked, preferred_element_type=jnp.float32)
    return total


def halving_scatter(x, names):
    sizes = [lax.axis_size(n) for n in names]
    labels = []
    for name, size in zip(names, sizes):
        bits = size.bit_length() - 1
        labels += [(name, j) for j in reversed(range(bits))]
    rows = x.shape[0] // math.prod(sizes)
    x = x.reshape((2,) * len(labels) + (rows,) + x.shape[1:])
    for name, size in reversed(list(zip(names, sizes))):
        for j in range(size.bit_length() - 1):
            pos = labels.index((name, j))
            bit = (lax.axis_index(name) >> j) & 1
            mine = lax.dynamic_index_in_dim(x, bit, axis=pos, keepdims=False)
            other = lax.dynamic_index_in_dim(x, 1 - bit, axis=pos, keepdims=False)
            perm = [(i, i ^ (1 << j)) for i in range(size)]
            x = mine + lax.ppermute(other, name, perm)
            labels.pop(pos)
    return x


def doubling_gather(x, names):
    for name in reversed(names):
        size = lax.axis_size(name)
        for j in range(size.bit_length() - 1):
            perm = [(i, i ^ (1 << j)) for i in range(size)]
            x = jnp.concatenate([x, lax.ppermute(x, name, perm)], axis=0)
    return x


def second_grad_rows(hidden_all, cot_all, names, total_rows):
    count, chans, depth, side = hidden_all.shape[0], hidden_all.shape[1], hidden_all.shape[2], hidden_all.shape[3]
    shards = math.prod(lax.axis_size(n) for n in names)
    rows = total_rows // shards
    index = 0
    for name in names:
        index = index * lax.axis_size(name) + lax.axis_index(name)
    first = index * rows
    tap0 = first // chans
    taps = min(27, (rows + 2 * chans - 2) // chans)
    padded = jnp.pad(hidden_all, ((0, 0), (0, 0), (1, 1), (1, 1), (1, 1)))
    pieces = []
    for slot in range(taps):
        tap = jnp.minimum(tap0 + slot, 26)
        window = lax.dynamic_slice(
            padded, (0, 0, tap // 9, (tap // 3) % 3, tap % 3), (count, chans, depth, side, side)
        ).reshape(count, chans, depth * side * side)
        pieces.append(
            lax.dot_general(
                window, cot_all, (((0, 2), (0, 2)), ((), ())), preferred_element_type=jnp.float32
            )
        )
    stacked = jnp.concatenate(pieces, axis=0)
    return lax.dynamic_slice_in_dim(stacked, first - tap0 * chans, rows, 0)


def ordered_gather(x, name):
    size = lax.axis_size(name)
    index = lax.axis_index(name)
    x = x[None]
    for j in range(size.bit_length() - 1):
        got = lax.ppermute(x, name, [(i, i ^ (1 << j)) for i in range(size)])
        low = ((index >> j) & 1) == 0
        x = jnp.where(low, jnp.concatenate([x, got]), jnp.concatenate([got, x]))
    return x


def block_local(volumes, cotangent, first_weight, second_weight):
    per, chans, planes = volumes.shape[1], volumes.shape[2], volumes.shape[3]
    half_c = chans // lax.axis_size("ch")
    pair_index = lax.axis_index("ch")
    half_o = first_weight.shape[1]
    spaces, subs = lax.axis_size("space"), lax.axis_size("sub")
    depth = spaces * planes
    half_z, half_s = (depth // 2, XY // 2)
    voxels = half_z * half_s * half_s
    factor = 1.0 / math.sqrt(spaces * subs * voxels)
    all_first = lax.all_gather(first_weight, "ch", axis=1, tiled=True)
    width = all_first.shape[1]
    vol_size = volumes.size
    flat = jnp.concatenate([volumes.reshape(-1), cotangent.reshape(-1)])
    near = ordered_gather(flat, "space")
    own = lax.dynamic_index_in_dim(
        near[:, :vol_size].reshape(spaces, per, chans, planes, XY * XY),
        lax.axis_index("space"),
        axis=1,
        keepdims=False,
    )
    sample = own.transpose(1, 0, 2, 3).reshape(chans, depth, XY * XY)
    cols = to_depth(sample, XY)
    pre = lax.dot_general(
        all_first, cols, (((0,), (0,)), ((), ())), preferred_element_type=jnp.float32
    )
    grid = jax.nn.silu(pre).astype(jnp.bfloat16).reshape(width, half_z, half_s, half_s)
    out = conv_forward(grid, second_weight)
    block_out = out.astype(jnp.bfloat16).reshape(1, 1, half_o, half_z, half_s * half_s)
    cot = cotangent.reshape(half_o, voxels)
    cot_grid = cot.reshape(half_o, half_z, half_s, half_s)
    local_rows = second_weight.reshape(27, width, half_o)
    hidden_grad = halving_scatter(conv_back(cot_grid, local_rows), ("ch",))
    pre_half = lax.dynamic_slice_in_dim(pre, pair_index * half_o, half_o, 0)
    pre_grad = (hidden_grad * silu_slope(pre_half)).astype(jnp.bfloat16)
    grad_first = (
        lax.dot_general(
            cols, pre_grad, (((1,), (1,)), ((), ())), preferred_element_type=jnp.float32
        )
        * factor
    )
    all_pre_grad = lax.all_gather(pre_grad, "ch", axis=0, tiled=True)
    first_rows = lax.dynamic_slice_in_dim(
        all_first.reshape(8, chans, width), pair_index * half_c, half_c, 1
    )
    grad_cols = jnp.dot(
        first_rows.reshape(8 * half_c, width), all_pre_grad, preferred_element_type=jnp.float32
    )
    grad_sample = from_depth(grad_cols, half_c, depth, XY).astype(jnp.bfloat16)
    volume_grad = lax.all_to_all(
        grad_sample.reshape(1, 1, half_c, depth, XY * XY),
        "space",
        split_axis=3,
        concat_axis=1,
        tiled=True,
    )
    first_grad = halving_scatter(grad_first, ("space", "sub"))
    far = ordered_gather(near, "sub")
    count = subs * spaces
    vols = far[:, :, :vol_size].reshape(subs, spaces, per, chans, planes, XY * XY)
    samples = vols.transpose(0, 2, 3, 1, 4, 5).reshape(subs * per, chans, depth, XY * XY)
    cols_all = jax.vmap(lambda s: to_depth(s, XY))(samples)
    pre_all = jnp.einsum("ro,nrv->nov", all_first, cols_all, preferred_element_type=jnp.float32)
    hidden_all = jax.nn.silu(pre_all).astype(jnp.bfloat16)
    cot_all = far[:, :, vol_size:].reshape(count, half_o, voxels)
    second_grad = (
        second_grad_rows(
            hidden_all.reshape(count, width, half_z, half_s, half_s),
            cot_all,
            ("space", "sub"),
            second_weight.shape[0],
        )
        * factor
    )
    return (block_out, volume_grad, first_grad, second_grad)


def silu_slope(pre):
    sig = jax.nn.sigmoid(pre)
    return sig * (1.0 + pre * (1.0 - sig))


def block(volumes, cotangent, first_weight, second_weight):
    shards = lax.axis_size("space") * lax.axis_size("sub")
    local_bytes = (volumes.size + cotangent.size) * 2
    if volumes.shape[1] == lax.axis_size("space") and shards * local_bytes <= 1 << 22:
        return block_local(volumes, cotangent, first_weight, second_weight)
    chans = volumes.shape[2]
    half_c = chans // lax.axis_size("ch")
    pair_index = lax.axis_index("ch")
    half_o = first_weight.shape[1]
    sample = lax.all_to_all(volumes, "space", split_axis=1, concat_axis=3, tiled=True)
    depth = sample.shape[3]
    sample = sample.reshape(chans, depth, XY * XY)
    half_z, half_s = (depth // 2, XY // 2)
    voxels = half_z * half_s * half_s
    cols = to_depth(sample, XY)
    pre = lax.dot_general(
        first_weight, cols, (((0,), (0,)), ((), ())), preferred_element_type=jnp.float32
    )
    hidden = jax.nn.silu(pre).astype(jnp.bfloat16)
    grid = lax.all_gather(hidden.reshape(half_o, half_z, half_s, half_s), "ch", axis=0, tiled=True)
    width = grid.shape[0]
    out = conv_forward(grid, second_weight)
    block_out = out.astype(jnp.bfloat16).reshape(1, 1, half_o, half_z, half_s * half_s)
    cot = cotangent.reshape(half_o, voxels)
    factor = 1.0 / math.sqrt(lax.axis_size("space") * lax.axis_size("sub") * voxels)
    shards = lax.axis_size("space") * lax.axis_size("sub")
    gather_second = shards * (width + half_o) * voxels * 2 <= 1 << 22
    if gather_second:
        both = doubling_gather(
            jnp.concatenate([grid.reshape(width, voxels), cot], axis=0)[None], ("space", "sub")
        )
        grad_second = (
            second_grad_rows(
                both[:, :width].reshape(both.shape[0], width, half_z, half_s, half_s),
                both[:, width:],
                ("space", "sub"),
                second_weight.shape[0],
            )
            * factor
        )
    else:
        grad_second = conv_weight_grad(grid, cot) * factor
    cot_grid = cot.reshape(half_o, half_z, half_s, half_s)
    local_rows = second_weight.reshape(27, width, half_o)
    hidden_grad = halving_scatter(conv_back(cot_grid, local_rows), ("ch",))
    pre_grad = (hidden_grad * silu_slope(pre)).astype(jnp.bfloat16)
    grad_first = (
        lax.dot_general(
            cols, pre_grad, (((1,), (1,)), ((), ())), preferred_element_type=jnp.float32
        )
        * factor
    )
    all_pre_grad = lax.all_gather(pre_grad, "ch", axis=0, tiled=True)
    all_first = lax.all_gather(first_weight, "ch", axis=1, tiled=True)
    first_rows = lax.dynamic_slice_in_dim(
        all_first.reshape(8, chans, width), pair_index * half_c, half_c, 1
    )
    grad_cols = jnp.dot(
        first_rows.reshape(8 * half_c, width), all_pre_grad, preferred_element_type=jnp.float32
    )
    grad_sample = from_depth(grad_cols, half_c, depth, XY).astype(jnp.bfloat16)
    volume_grad = lax.all_to_all(
        grad_sample.reshape(1, 1, half_c, depth, XY * XY),
        "space",
        split_axis=3,
        concat_axis=1,
        tiled=True,
    )
    first_grad = halving_scatter(grad_first, ("space", "sub"))
    second_grad = (
        grad_second if gather_second else halving_scatter(grad_second, ("space", "sub"))
    )
    return (block_out, volume_grad, first_grad, second_grad)


def solution(mesh):
    return step_of(mesh)


def step_of(mesh):
    return jax.shard_map(
        block,
        mesh=mesh,
        in_specs=(
            P(("groups", "sub"), None, None, "space", None),
            P(("groups", "sub"), "space", "ch", None, None),
            P(None, "ch"),
            P(None, "ch"),
        ),
        out_specs=(
            P(("groups", "sub"), "space", "ch", None, None),
            P(("groups", "sub"), None, "ch", "space", None),
            P(("space", "sub"), ("groups", "ch")),
            P(("space", "sub"), ("groups", "ch")),
        ),
        check_vma=False,
    )
```

```python
import math

import jax
import jax.numpy as jnp
from jax import lax
from jax.sharding import PartitionSpec as P


XY = 16


def to_depth(sample, side):
    chans, depth = (sample.shape[0], sample.shape[1])
    blocks = sample.reshape(chans, depth // 2, 2, side // 2, 2, side // 2, 2)
    blocks = blocks.transpose(2, 4, 6, 0, 1, 3, 5)
    return blocks.reshape(8 * chans, depth // 2 * (side // 2) * (side // 2))


def from_depth(cols, chans, depth, side):
    blocks = cols.reshape(2, 2, 2, chans, depth // 2, side // 2, side // 2)
    blocks = blocks.transpose(3, 4, 0, 5, 1, 6, 2)
    return blocks.reshape(chans, depth, side * side)


def plane_stack(padded, plane, depth, side, flip):
    chans = padded.shape[0]
    windows = []
    for inner in range(9):
        b, c = (inner // 3, inner % 3)
        if flip:
            window = padded[
                :, 2 - plane : 2 - plane + depth, 2 - b : 2 - b + side, 2 - c : 2 - c + side
            ]
        else:
            window = padded[:, plane : plane + depth, b : b + side, c : c + side]
        windows.append(window.reshape(chans, depth * side * side))
    return jnp.concatenate(windows, axis=0)


def conv_forward(hidden, weight):
    chans, depth, side = (hidden.shape[0], hidden.shape[1], hidden.shape[2])
    padded = jnp.pad(hidden, ((0, 0), (1, 1), (1, 1), (1, 1)))
    total = jnp.zeros((weight.shape[1], depth * side * side), jnp.float32)
    for plane in range(3):
        stacked = plane_stack(padded, plane, depth, side, False)
        piece = weight[plane * 9 * chans : (plane + 1) * 9 * chans]
        total = total + lax.dot_general(
            piece, stacked, (((0,), (0,)), ((), ())), preferred_element_type=jnp.float32
        )
    return total


def conv_weight_grad(hidden, cot):
    depth, side = (hidden.shape[1], hidden.shape[2])
    padded = jnp.pad(hidden, ((0, 0), (1, 1), (1, 1), (1, 1)))
    pieces = []
    for plane in range(3):
        stacked = plane_stack(padded, plane, depth, side, False)
        pieces.append(
            lax.dot_general(
                stacked, cot, (((1,), (1,)), ((), ())), preferred_element_type=jnp.float32
            )
        )
    return jnp.concatenate(pieces, axis=0)


def conv_back(cot, weight_rows):
    depth, side = (cot.shape[1], cot.shape[2])
    padded = jnp.pad(cot, ((0, 0), (1, 1), (1, 1), (1, 1)))
    total = jnp.zeros((weight_rows.shape[1], depth * side * side), jnp.float32)
    for plane in range(3):
        stacked = plane_stack(padded, plane, depth, side, True)
        group = weight_rows[plane * 9 : (plane + 1) * 9]
        lhs = group.transpose(1, 0, 2).reshape(group.shape[1], 9 * group.shape[2])
        total = total + jnp.dot(lhs, stacked, preferred_element_type=jnp.float32)
    return total


def halving_scatter(x, names):
    sizes = [lax.axis_size(n) for n in names]
    labels = []
    for name, size in zip(names, sizes):
        bits = size.bit_length() - 1
        labels += [(name, j) for j in reversed(range(bits))]
    rows = x.shape[0] // math.prod(sizes)
    x = x.reshape((2,) * len(labels) + (rows,) + x.shape[1:])
    for name, size in reversed(list(zip(names, sizes))):
        for j in range(size.bit_length() - 1):
            pos = labels.index((name, j))
            bit = (lax.axis_index(name) >> j) & 1
            mine = lax.dynamic_index_in_dim(x, bit, axis=pos, keepdims=False)
            other = lax.dynamic_index_in_dim(x, 1 - bit, axis=pos, keepdims=False)
            perm = [(i, i ^ (1 << j)) for i in range(size)]
            x = mine + lax.ppermute(other, name, perm)
            labels.pop(pos)
    return x


def second_grad_rows(hidden_all, cot_all, names, total_rows):
    count, chans, depth, side = hidden_all.shape[0], hidden_all.shape[1], hidden_all.shape[2], hidden_all.shape[3]
    shards = math.prod(lax.axis_size(n) for n in names)
    rows = total_rows // shards
    index = 0
    for name in names:
        index = index * lax.axis_size(name) + lax.axis_index(name)
    first = index * rows
    tap0 = first // chans
    taps = min(27, (rows + 2 * chans - 2) // chans)
    padded = jnp.pad(hidden_all, ((0, 0), (0, 0), (1, 1), (1, 1), (1, 1)))
    pieces = []
    for slot in range(taps):
        tap = jnp.minimum(tap0 + slot, 26)
        window = lax.dynamic_slice(
            padded, (0, 0, tap // 9, (tap // 3) % 3, tap % 3), (count, chans, depth, side, side)
        ).reshape(count, chans, depth * side * side)
        pieces.append(
            lax.dot_general(
                window, cot_all, (((0, 2), (0, 2)), ((), ())), preferred_element_type=jnp.float32
            )
        )
    stacked = jnp.concatenate(pieces, axis=0)
    return lax.dynamic_slice_in_dim(stacked, first - tap0 * chans, rows, 0)


def exchange_gather(x, names):
    count = math.prod(lax.axis_size(n) for n in names)
    copies = jnp.broadcast_to(x[None], (count,) + x.shape)
    return lax.all_to_all(copies, names, 0, 0, tiled=True)


def exchange_scatter(x, names):
    count = math.prod(lax.axis_size(n) for n in names)
    if count > 8:
        return halving_scatter(x, names)
    blocks = x.reshape((count, x.shape[0] // count) + x.shape[1:])
    return lax.all_to_all(blocks, names, 0, 0, tiled=True).sum(axis=0)


def silu_slope(pre):
    sig = jax.nn.sigmoid(pre)
    return sig * (1.0 + pre * (1.0 - sig))


def block(volumes, cotangent, first_weight, second_weight):
    chans = volumes.shape[2]
    half_c = chans // lax.axis_size("ch")
    pair_index = lax.axis_index("ch")
    half_o = first_weight.shape[1]
    sample = lax.all_to_all(volumes, "space", split_axis=1, concat_axis=3, tiled=True)
    depth = sample.shape[3]
    sample = sample.reshape(chans, depth, XY * XY)
    half_z, half_s = (depth // 2, XY // 2)
    voxels = half_z * half_s * half_s
    cols = to_depth(sample, XY)
    pre = lax.dot_general(
        first_weight, cols, (((0,), (0,)), ((), ())), preferred_element_type=jnp.float32
    )
    hidden = jax.nn.silu(pre).astype(jnp.bfloat16)
    grid = lax.all_gather(hidden.reshape(half_o, half_z, half_s, half_s), "ch", axis=0, tiled=True)
    width = grid.shape[0]
    out = conv_forward(grid, second_weight)
    block_out = out.astype(jnp.bfloat16).reshape(1, 1, half_o, half_z, half_s * half_s)
    cot = cotangent.reshape(half_o, voxels)
    factor = 1.0 / math.sqrt(lax.axis_size("space") * lax.axis_size("sub") * voxels)
    shards = lax.axis_size("space") * lax.axis_size("sub")
    gather_second = shards * (width + half_o) * voxels * 2 <= 1 << 22
    if gather_second:
        both = exchange_gather(
            jnp.concatenate([grid.reshape(width, voxels), cot], axis=0), ("space", "sub")
        )
        grad_second = (
            second_grad_rows(
                both[:, :width].reshape(both.shape[0], width, half_z, half_s, half_s),
                both[:, width:],
                ("space", "sub"),
                second_weight.shape[0],
            )
            * factor
        )
    else:
        grad_second = conv_weight_grad(grid, cot) * factor
    cot_grid = cot.reshape(half_o, half_z, half_s, half_s)
    local_rows = second_weight.reshape(27, width, half_o)
    hidden_grad = halving_scatter(conv_back(cot_grid, local_rows), ("ch",))
    pre_grad = (hidden_grad * silu_slope(pre)).astype(jnp.bfloat16)
    grad_first = (
        lax.dot_general(
            cols, pre_grad, (((1,), (1,)), ((), ())), preferred_element_type=jnp.float32
        )
        * factor
    )
    all_pre_grad = lax.all_gather(pre_grad, "ch", axis=0, tiled=True)
    all_first = lax.all_gather(first_weight, "ch", axis=1, tiled=True)
    first_rows = lax.dynamic_slice_in_dim(
        all_first.reshape(8, chans, width), pair_index * half_c, half_c, 1
    )
    grad_cols = jnp.dot(
        first_rows.reshape(8 * half_c, width), all_pre_grad, preferred_element_type=jnp.float32
    )
    grad_sample = from_depth(grad_cols, half_c, depth, XY).astype(jnp.bfloat16)
    volume_grad = lax.all_to_all(
        grad_sample.reshape(1, 1, half_c, depth, XY * XY),
        "space",
        split_axis=3,
        concat_axis=1,
        tiled=True,
    )
    first_grad = exchange_scatter(grad_first, ("space", "sub"))
    second_grad = (
        grad_second if gather_second else halving_scatter(grad_second, ("space", "sub"))
    )
    return (block_out, volume_grad, first_grad, second_grad)


def solution(mesh):
    return step_of(mesh)


def step_of(mesh):
    return jax.shard_map(
        block,
        mesh=mesh,
        in_specs=(
            P(("groups", "sub"), None, None, "space", None),
            P(("groups", "sub"), "space", "ch", None, None),
            P(None, "ch"),
            P(None, "ch"),
        ),
        out_specs=(
            P(("groups", "sub"), "space", "ch", None, None),
            P(("groups", "sub"), None, "ch", "space", None),
            P(("space", "sub"), ("groups", "ch")),
            P(("space", "sub"), ("groups", "ch")),
        ),
        check_vma=False,
    )
```

```python
import math

import jax
import jax.numpy as jnp
from jax import lax
from jax.sharding import PartitionSpec as P


XY = 16


def to_depth(sample, side):
    chans, depth = (sample.shape[0], sample.shape[1])
    blocks = sample.reshape(chans, depth // 2, 2, side // 2, 2, side // 2, 2)
    blocks = blocks.transpose(2, 4, 6, 0, 1, 3, 5)
    return blocks.reshape(8 * chans, depth // 2 * (side // 2) * (side // 2))


def from_depth(cols, chans, depth, side):
    blocks = cols.reshape(2, 2, 2, chans, depth // 2, side // 2, side // 2)
    blocks = blocks.transpose(3, 4, 0, 5, 1, 6, 2)
    return blocks.reshape(chans, depth, side * side)


def plane_stack(padded, plane, depth, side, flip):
    chans = padded.shape[0]
    windows = []
    for inner in range(9):
        b, c = (inner // 3, inner % 3)
        if flip:
            window = padded[
                :, 2 - plane : 2 - plane + depth, 2 - b : 2 - b + side, 2 - c : 2 - c + side
            ]
        else:
            window = padded[:, plane : plane + depth, b : b + side, c : c + side]
        windows.append(window.reshape(chans, depth * side * side))
    return jnp.concatenate(windows, axis=0)


def conv_forward(hidden, weight):
    chans, depth, side = (hidden.shape[0], hidden.shape[1], hidden.shape[2])
    padded = jnp.pad(hidden, ((0, 0), (1, 1), (1, 1), (1, 1)))
    total = jnp.zeros((weight.shape[1], depth * side * side), jnp.float32)
    for plane in range(3):
        stacked = plane_stack(padded, plane, depth, side, False)
        piece = weight[plane * 9 * chans : (plane + 1) * 9 * chans]
        total = total + lax.dot_general(
            piece, stacked, (((0,), (0,)), ((), ())), preferred_element_type=jnp.float32
        )
    return total


def conv_weight_grad(hidden, cot):
    depth, side = (hidden.shape[1], hidden.shape[2])
    padded = jnp.pad(hidden, ((0, 0), (1, 1), (1, 1), (1, 1)))
    pieces = []
    for plane in range(3):
        stacked = plane_stack(padded, plane, depth, side, False)
        pieces.append(
            lax.dot_general(
                stacked, cot, (((1,), (1,)), ((), ())), preferred_element_type=jnp.float32
            )
        )
    return jnp.concatenate(pieces, axis=0)


def conv_back(cot, weight_rows):
    depth, side = (cot.shape[1], cot.shape[2])
    padded = jnp.pad(cot, ((0, 0), (1, 1), (1, 1), (1, 1)))
    total = jnp.zeros((weight_rows.shape[1], depth * side * side), jnp.float32)
    for plane in range(3):
        stacked = plane_stack(padded, plane, depth, side, True)
        group = weight_rows[plane * 9 : (plane + 1) * 9]
        lhs = group.transpose(1, 0, 2).reshape(group.shape[1], 9 * group.shape[2])
        total = total + jnp.dot(lhs, stacked, preferred_element_type=jnp.float32)
    return total


def halving_scatter(x, names):
    sizes = [lax.axis_size(n) for n in names]
    labels = []
    for name, size in zip(names, sizes):
        bits = size.bit_length() - 1
        labels += [(name, j) for j in reversed(range(bits))]
    rows = x.shape[0] // math.prod(sizes)
    x = x.reshape((2,) * len(labels) + (rows,) + x.shape[1:])
    for name, size in reversed(list(zip(names, sizes))):
        for j in range(size.bit_length() - 1):
            pos = labels.index((name, j))
            bit = (lax.axis_index(name) >> j) & 1
            mine = lax.dynamic_index_in_dim(x, bit, axis=pos, keepdims=False)
            other = lax.dynamic_index_in_dim(x, 1 - bit, axis=pos, keepdims=False)
            perm = [(i, i ^ (1 << j)) for i in range(size)]
            x = mine + lax.ppermute(other, name, perm)
            labels.pop(pos)
    return x


def doubling_gather(x, names):
    for name in names:
        size = lax.axis_size(name)
        for j in reversed(range(size.bit_length() - 1)):
            perm = [(i, i ^ (1 << j)) for i in range(size)]
            x = jnp.concatenate([x, lax.ppermute(x, name, perm)], axis=0)
    return x


def second_grad_rows(hidden_all, cot_all, names, total_rows):
    count, chans, depth, side = hidden_all.shape[0], hidden_all.shape[1], hidden_all.shape[2], hidden_all.shape[3]
    shards = math.prod(lax.axis_size(n) for n in names)
    rows = total_rows // shards
    index = 0
    for name in names:
        index = index * lax.axis_size(name) + lax.axis_index(name)
    first = index * rows
    tap0 = first // chans
    taps = min(27, (rows + 2 * chans - 2) // chans)
    padded = jnp.pad(hidden_all, ((0, 0), (0, 0), (1, 1), (1, 1), (1, 1)))
    pieces = []
    for slot in range(taps):
        tap = jnp.minimum(tap0 + slot, 26)
        window = lax.dynamic_slice(
            padded, (0, 0, tap // 9, (tap // 3) % 3, tap % 3), (count, chans, depth, side, side)
        ).reshape(count, chans, depth * side * side)
        pieces.append(
            lax.dot_general(
                window, cot_all, (((0, 2), (0, 2)), ((), ())), preferred_element_type=jnp.float32
            )
        )
    stacked = jnp.concatenate(pieces, axis=0)
    return lax.dynamic_slice_in_dim(stacked, first - tap0 * chans, rows, 0)


def silu_slope(pre):
    sig = jax.nn.sigmoid(pre)
    return sig * (1.0 + pre * (1.0 - sig))


def block(volumes, cotangent, first_weight, second_weight):
    chans = volumes.shape[2]
    half_c = chans // lax.axis_size("ch")
    pair_index = lax.axis_index("ch")
    half_o = first_weight.shape[1]
    sample = lax.all_to_all(volumes, "space", split_axis=1, concat_axis=3, tiled=True)
    depth = sample.shape[3]
    sample = sample.reshape(chans, depth, XY * XY)
    half_z, half_s = (depth // 2, XY // 2)
    voxels = half_z * half_s * half_s
    cols = to_depth(sample, XY)
    pre = lax.dot_general(
        first_weight, cols, (((0,), (0,)), ((), ())), preferred_element_type=jnp.float32
    )
    hidden = jax.nn.silu(pre).astype(jnp.bfloat16)
    grid = lax.all_gather(hidden.reshape(half_o, half_z, half_s, half_s), "ch", axis=0, tiled=True)
    width = grid.shape[0]
    out = conv_forward(grid, second_weight)
    block_out = out.astype(jnp.bfloat16).reshape(1, 1, half_o, half_z, half_s * half_s)
    cot = cotangent.reshape(half_o, voxels)
    factor = 1.0 / math.sqrt(lax.axis_size("space") * lax.axis_size("sub") * voxels)
    shards = lax.axis_size("space") * lax.axis_size("sub")
    gather_second = shards * (width + half_o) * voxels * 2 <= 1 << 22
    if gather_second:
        both = doubling_gather(
            jnp.concatenate([grid.reshape(width, voxels), cot], axis=0)[None], ("space", "sub")
        )
        grad_second = (
            second_grad_rows(
                both[:, :width].reshape(both.shape[0], width, half_z, half_s, half_s),
                both[:, width:],
                ("space", "sub"),
                second_weight.shape[0],
            )
            * factor
        )
    else:
        grad_second = conv_weight_grad(grid, cot) * factor
    cot_grid = cot.reshape(half_o, half_z, half_s, half_s)
    local_rows = second_weight.reshape(27, width, half_o)
    hidden_grad = halving_scatter(conv_back(cot_grid, local_rows), ("ch",))
    pre_grad = (hidden_grad * silu_slope(pre)).astype(jnp.bfloat16)
    grad_first = (
        lax.dot_general(
            cols, pre_grad, (((1,), (1,)), ((), ())), preferred_element_type=jnp.float32
        )
        * factor
    )
    all_pre_grad = lax.all_gather(pre_grad, "ch", axis=0, tiled=True)
    all_first = lax.all_gather(first_weight, "ch", axis=1, tiled=True)
    first_rows = lax.dynamic_slice_in_dim(
        all_first.reshape(8, chans, width), pair_index * half_c, half_c, 1
    )
    grad_cols = jnp.dot(
        first_rows.reshape(8 * half_c, width), all_pre_grad, preferred_element_type=jnp.float32
    )
    grad_sample = from_depth(grad_cols, half_c, depth, XY).astype(jnp.bfloat16)
    volume_grad = lax.all_to_all(
        grad_sample.reshape(1, 1, half_c, depth, XY * XY),
        "space",
        split_axis=3,
        concat_axis=1,
        tiled=True,
    )
    first_grad = halving_scatter(grad_first, ("space", "sub"))
    second_grad = (
        grad_second if gather_second else halving_scatter(grad_second, ("space", "sub"))
    )
    return (block_out, volume_grad, first_grad, second_grad)


def solution(mesh):
    return step_of(mesh)


def step_of(mesh):
    return jax.shard_map(
        block,
        mesh=mesh,
        in_specs=(
            P(("groups", "sub"), None, None, "space", None),
            P(("groups", "sub"), "space", "ch", None, None),
            P(None, "ch"),
            P(None, "ch"),
        ),
        out_specs=(
            P(("groups", "sub"), "space", "ch", None, None),
            P(("groups", "sub"), None, "ch", "space", None),
            P(("space", "sub"), ("groups", "ch")),
            P(("space", "sub"), ("groups", "ch")),
        ),
        check_vma=False,
    )
```

```python
import math

import jax
import jax.numpy as jnp
from jax import lax
from jax.sharding import PartitionSpec as P


XY = 16


def to_depth(sample, side):
    chans, depth = (sample.shape[0], sample.shape[1])
    blocks = sample.reshape(chans, depth // 2, 2, side // 2, 2, side // 2, 2)
    blocks = blocks.transpose(2, 4, 6, 0, 1, 3, 5)
    return blocks.reshape(8 * chans, depth // 2 * (side // 2) * (side // 2))


def from_depth(cols, chans, depth, side):
    blocks = cols.reshape(2, 2, 2, chans, depth // 2, side // 2, side // 2)
    blocks = blocks.transpose(3, 4, 0, 5, 1, 6, 2)
    return blocks.reshape(chans, depth, side * side)


def plane_stack(padded, plane, depth, side, flip):
    chans = padded.shape[0]
    windows = []
    for inner in range(9):
        b, c = (inner // 3, inner % 3)
        if flip:
            window = padded[
                :, 2 - plane : 2 - plane + depth, 2 - b : 2 - b + side, 2 - c : 2 - c + side
            ]
        else:
            window = padded[:, plane : plane + depth, b : b + side, c : c + side]
        windows.append(window.reshape(chans, depth * side * side))
    return jnp.concatenate(windows, axis=0)


def conv_forward(hidden, weight):
    chans, depth, side = (hidden.shape[0], hidden.shape[1], hidden.shape[2])
    padded = jnp.pad(hidden, ((0, 0), (1, 1), (1, 1), (1, 1)))
    total = jnp.zeros((weight.shape[1], depth * side * side), jnp.float32)
    for plane in range(3):
        stacked = plane_stack(padded, plane, depth, side, False)
        piece = weight[plane * 9 * chans : (plane + 1) * 9 * chans]
        total = total + lax.dot_general(
            piece, stacked, (((0,), (0,)), ((), ())), preferred_element_type=jnp.float32
        )
    return total


def conv_weight_grad(hidden, cot):
    depth, side = (hidden.shape[1], hidden.shape[2])
    padded = jnp.pad(hidden, ((0, 0), (1, 1), (1, 1), (1, 1)))
    pieces = []
    for plane in range(3):
        stacked = plane_stack(padded, plane, depth, side, False)
        pieces.append(
            lax.dot_general(
                stacked, cot, (((1,), (1,)), ((), ())), preferred_element_type=jnp.float32
            )
        )
    return jnp.concatenate(pieces, axis=0)


def conv_back(cot, weight_rows):
    depth, side = (cot.shape[1], cot.shape[2])
    padded = jnp.pad(cot, ((0, 0), (1, 1), (1, 1), (1, 1)))
    total = jnp.zeros((weight_rows.shape[1], depth * side * side), jnp.float32)
    for plane in range(3):
        stacked = plane_stack(padded, plane, depth, side, True)
        group = weight_rows[plane * 9 : (plane + 1) * 9]
        lhs = group.transpose(1, 0, 2).reshape(group.shape[1], 9 * group.shape[2])
        total = total + jnp.dot(lhs, stacked, preferred_element_type=jnp.float32)
    return total


def halving_scatter(x, names):
    sizes = [lax.axis_size(n) for n in names]
    labels = []
    for name, size in zip(names, sizes):
        bits = size.bit_length() - 1
        labels += [(name, j) for j in reversed(range(bits))]
    rows = x.shape[0] // math.prod(sizes)
    x = x.reshape((2,) * len(labels) + (rows,) + x.shape[1:])
    for name, size in reversed(list(zip(names, sizes))):
        for j in range(size.bit_length() - 1):
            pos = labels.index((name, j))
            bit = (lax.axis_index(name) >> j) & 1
            mine = lax.dynamic_index_in_dim(x, bit, axis=pos, keepdims=False)
            other = lax.dynamic_index_in_dim(x, 1 - bit, axis=pos, keepdims=False)
            perm = [(i, i ^ (1 << j)) for i in range(size)]
            x = mine + lax.ppermute(other, name, perm)
            labels.pop(pos)
    return x


def second_grad_rows(hidden_all, cot_all, names, total_rows):
    count, chans, depth, side = hidden_all.shape[0], hidden_all.shape[1], hidden_all.shape[2], hidden_all.shape[3]
    shards = math.prod(lax.axis_size(n) for n in names)
    rows = total_rows // shards
    index = 0
    for name in names:
        index = index * lax.axis_size(name) + lax.axis_index(name)
    first = index * rows
    tap0 = first // chans
    taps = min(27, (rows + 2 * chans - 2) // chans)
    padded = jnp.pad(hidden_all, ((0, 0), (0, 0), (1, 1), (1, 1), (1, 1)))
    pieces = []
    for slot in range(taps):
        tap = jnp.minimum(tap0 + slot, 26)
        window = lax.dynamic_slice(
            padded, (0, 0, tap // 9, (tap // 3) % 3, tap % 3), (count, chans, depth, side, side)
        ).reshape(count, chans, depth * side * side)
        pieces.append(
            lax.dot_general(
                window, cot_all, (((0, 2), (0, 2)), ((), ())), preferred_element_type=jnp.float32
            )
        )
    stacked = jnp.concatenate(pieces, axis=0)
    return lax.dynamic_slice_in_dim(stacked, first - tap0 * chans, rows, 0)


def fused_chain(x, y, names):
    sizes = [lax.axis_size(n) for n in names]
    labels = []
    for name, size in zip(names, sizes):
        labels += [(name, j) for j in reversed(range(size.bit_length() - 1))]
    rows = y.shape[0] // math.prod(sizes)
    y = y.reshape((2,) * len(labels) + (rows,) + y.shape[1:])
    lanes = x.shape[-1]
    x = x[None]
    for name, size in zip(names, sizes):
        for j in reversed(range(size.bit_length() - 1)):
            pos = labels.index((name, j))
            bit = (lax.axis_index(name) >> j) & 1
            mine = lax.dynamic_index_in_dim(y, bit, axis=pos, keepdims=False)
            other = lax.dynamic_index_in_dim(y, 1 - bit, axis=pos, keepdims=False)
            high = other.astype(jnp.bfloat16)
            low = (other - high.astype(jnp.float32)).astype(jnp.bfloat16)
            message = jnp.concatenate(
                [x.reshape(-1, lanes), high.reshape(-1, lanes), low.reshape(-1, lanes)], axis=0
            )
            perm = [(i, i ^ (1 << j)) for i in range(size)]
            got = lax.ppermute(message, name, perm)
            kept, part = x.size // lanes, high.size // lanes
            x = jnp.concatenate([x, got[:kept].reshape(x.shape)], axis=0)
            y = (
                mine
                + got[kept : kept + part].reshape(high.shape).astype(jnp.float32)
                + got[kept + part :].reshape(high.shape).astype(jnp.float32)
            )
            labels.pop(pos)
    return x, y


def silu_slope(pre):
    sig = jax.nn.sigmoid(pre)
    return sig * (1.0 + pre * (1.0 - sig))


def block(volumes, cotangent, first_weight, second_weight):
    chans = volumes.shape[2]
    half_c = chans // lax.axis_size("ch")
    pair_index = lax.axis_index("ch")
    half_o = first_weight.shape[1]
    sample = lax.all_to_all(volumes, "space", split_axis=1, concat_axis=3, tiled=True)
    depth = sample.shape[3]
    sample = sample.reshape(chans, depth, XY * XY)
    half_z, half_s = (depth // 2, XY // 2)
    voxels = half_z * half_s * half_s
    cols = to_depth(sample, XY)
    pre = lax.dot_general(
        first_weight, cols, (((0,), (0,)), ((), ())), preferred_element_type=jnp.float32
    )
    hidden = jax.nn.silu(pre).astype(jnp.bfloat16)
    grid = lax.all_gather(hidden.reshape(half_o, half_z, half_s, half_s), "ch", axis=0, tiled=True)
    width = grid.shape[0]
    out = conv_forward(grid, second_weight)
    block_out = out.astype(jnp.bfloat16).reshape(1, 1, half_o, half_z, half_s * half_s)
    cot = cotangent.reshape(half_o, voxels)
    factor = 1.0 / math.sqrt(lax.axis_size("space") * lax.axis_size("sub") * voxels)
    cot_grid = cot.reshape(half_o, half_z, half_s, half_s)
    local_rows = second_weight.reshape(27, width, half_o)
    hidden_grad = halving_scatter(conv_back(cot_grid, local_rows), ("ch",))
    pre_grad = (hidden_grad * silu_slope(pre)).astype(jnp.bfloat16)
    grad_first = (
        lax.dot_general(
            cols, pre_grad, (((1,), (1,)), ((), ())), preferred_element_type=jnp.float32
        )
        * factor
    )
    shards = lax.axis_size("space") * lax.axis_size("sub")
    gather_second = shards * (width + half_o) * voxels * 2 <= 1 << 22
    gather_second = gather_second and (grad_first.size // shards) % voxels == 0
    if gather_second:
        both, first_grad = fused_chain(
            jnp.concatenate([grid.reshape(width, voxels), cot], axis=0),
            grad_first,
            ("space", "sub"),
        )
        second_grad = (
            second_grad_rows(
                both[:, :width].reshape(both.shape[0], width, half_z, half_s, half_s),
                both[:, width:],
                ("space", "sub"),
                second_weight.shape[0],
            )
            * factor
        )
    else:
        grad_second = conv_weight_grad(grid, cot) * factor
        first_grad = halving_scatter(grad_first, ("space", "sub"))
        second_grad = halving_scatter(grad_second, ("space", "sub"))
    all_pre_grad = lax.all_gather(pre_grad, "ch", axis=0, tiled=True)
    all_first = lax.all_gather(first_weight, "ch", axis=1, tiled=True)
    first_rows = lax.dynamic_slice_in_dim(
        all_first.reshape(8, chans, width), pair_index * half_c, half_c, 1
    )
    grad_cols = jnp.dot(
        first_rows.reshape(8 * half_c, width), all_pre_grad, preferred_element_type=jnp.float32
    )
    grad_sample = from_depth(grad_cols, half_c, depth, XY).astype(jnp.bfloat16)
    volume_grad = lax.all_to_all(
        grad_sample.reshape(1, 1, half_c, depth, XY * XY),
        "space",
        split_axis=3,
        concat_axis=1,
        tiled=True,
    )
    return (block_out, volume_grad, first_grad, second_grad)


def solution(mesh):
    return step_of(mesh)


def step_of(mesh):
    return jax.shard_map(
        block,
        mesh=mesh,
        in_specs=(
            P(("groups", "sub"), None, None, "space", None),
            P(("groups", "sub"), "space", "ch", None, None),
            P(None, "ch"),
            P(None, "ch"),
        ),
        out_specs=(
            P(("groups", "sub"), "space", "ch", None, None),
            P(("groups", "sub"), None, "ch", "space", None),
            P(("space", "sub"), ("groups", "ch")),
            P(("space", "sub"), ("groups", "ch")),
        ),
        check_vma=False,
    )
```

```python
import math

import jax
import jax.numpy as jnp
from jax import lax
from jax.sharding import PartitionSpec as P


XY = 16


def to_depth(sample, side):
    chans, depth = (sample.shape[0], sample.shape[1])
    blocks = sample.reshape(chans, depth // 2, 2, side // 2, 2, side // 2, 2)
    blocks = blocks.transpose(2, 4, 6, 0, 1, 3, 5)
    return blocks.reshape(8 * chans, depth // 2 * (side // 2) * (side // 2))


def from_depth(cols, chans, depth, side):
    blocks = cols.reshape(2, 2, 2, chans, depth // 2, side // 2, side // 2)
    blocks = blocks.transpose(3, 4, 0, 5, 1, 6, 2)
    return blocks.reshape(chans, depth, side * side)


def plane_stack(padded, plane, depth, side, flip):
    chans = padded.shape[0]
    windows = []
    for inner in range(9):
        b, c = (inner // 3, inner % 3)
        if flip:
            window = padded[
                :, 2 - plane : 2 - plane + depth, 2 - b : 2 - b + side, 2 - c : 2 - c + side
            ]
        else:
            window = padded[:, plane : plane + depth, b : b + side, c : c + side]
        windows.append(window.reshape(chans, depth * side * side))
    return jnp.concatenate(windows, axis=0)


def conv_forward(hidden, weight):
    chans, depth, side = (hidden.shape[0], hidden.shape[1], hidden.shape[2])
    padded = jnp.pad(hidden, ((0, 0), (1, 1), (1, 1), (1, 1)))
    total = jnp.zeros((weight.shape[1], depth * side * side), jnp.float32)
    for plane in range(3):
        stacked = plane_stack(padded, plane, depth, side, False)
        piece = weight[plane * 9 * chans : (plane + 1) * 9 * chans]
        total = total + lax.dot_general(
            piece, stacked, (((0,), (0,)), ((), ())), preferred_element_type=jnp.float32
        )
    return total


def conv_weight_grad(hidden, cot):
    depth, side = (hidden.shape[1], hidden.shape[2])
    padded = jnp.pad(hidden, ((0, 0), (1, 1), (1, 1), (1, 1)))
    pieces = []
    for plane in range(3):
        stacked = plane_stack(padded, plane, depth, side, False)
        pieces.append(
            lax.dot_general(
                stacked, cot, (((1,), (1,)), ((), ())), preferred_element_type=jnp.float32
            )
        )
    return jnp.concatenate(pieces, axis=0)


def conv_back(cot, weight_rows):
    depth, side = (cot.shape[1], cot.shape[2])
    padded = jnp.pad(cot, ((0, 0), (1, 1), (1, 1), (1, 1)))
    total = jnp.zeros((weight_rows.shape[1], depth * side * side), jnp.float32)
    for plane in range(3):
        stacked = plane_stack(padded, plane, depth, side, True)
        group = weight_rows[plane * 9 : (plane + 1) * 9]
        lhs = group.transpose(1, 0, 2).reshape(group.shape[1], 9 * group.shape[2])
        total = total + jnp.dot(lhs, stacked, preferred_element_type=jnp.float32)
    return total


def halving_scatter(x, names):
    sizes = [lax.axis_size(n) for n in names]
    labels = []
    for name, size in zip(names, sizes):
        bits = size.bit_length() - 1
        labels += [(name, j) for j in reversed(range(bits))]
    rows = x.shape[0] // math.prod(sizes)
    x = x.reshape((2,) * len(labels) + (rows,) + x.shape[1:])
    for name, size in reversed(list(zip(names, sizes))):
        for j in range(size.bit_length() - 1):
            pos = labels.index((name, j))
            bit = (lax.axis_index(name) >> j) & 1
            mine = lax.dynamic_index_in_dim(x, bit, axis=pos, keepdims=False)
            other = lax.dynamic_index_in_dim(x, 1 - bit, axis=pos, keepdims=False)
            perm = [(i, i ^ (1 << j)) for i in range(size)]
            x = mine + lax.ppermute(other, name, perm)
            labels.pop(pos)
    return x


def second_grad_rows(hidden_all, cot_all, names, total_rows):
    count, chans, depth, side = hidden_all.shape[0], hidden_all.shape[1], hidden_all.shape[2], hidden_all.shape[3]
    shards = math.prod(lax.axis_size(n) for n in names)
    rows = total_rows // shards
    index = 0
    for name in names:
        index = index * lax.axis_size(name) + lax.axis_index(name)
    first = index * rows
    tap0 = first // chans
    taps = min(27, (rows + 2 * chans - 2) // chans)
    padded = jnp.pad(hidden_all, ((0, 0), (0, 0), (1, 1), (1, 1), (1, 1)))
    pieces = []
    for slot in range(taps):
        tap = jnp.minimum(tap0 + slot, 26)
        window = lax.dynamic_slice(
            padded, (0, 0, tap // 9, (tap // 3) % 3, tap % 3), (count, chans, depth, side, side)
        ).reshape(count, chans, depth * side * side)
        pieces.append(
            lax.dot_general(
                window, cot_all, (((0, 2), (0, 2)), ((), ())), preferred_element_type=jnp.float32
            )
        )
    stacked = jnp.concatenate(pieces, axis=0)
    return lax.dynamic_slice_in_dim(stacked, first - tap0 * chans, rows, 0)


def fused_chain(x, y, names):
    sizes = [lax.axis_size(n) for n in names]
    labels = []
    for name, size in zip(names, sizes):
        labels += [(name, j) for j in reversed(range(size.bit_length() - 1))]
    rows = y.shape[0] // math.prod(sizes)
    y = y.reshape((2,) * len(labels) + (rows,) + y.shape[1:])
    lanes = x.shape[-1]
    x = x[None]
    for name, size in zip(names, sizes):
        for j in reversed(range(size.bit_length() - 1)):
            pos = labels.index((name, j))
            bit = (lax.axis_index(name) >> j) & 1
            mine = lax.dynamic_index_in_dim(y, bit, axis=pos, keepdims=False)
            other = lax.dynamic_index_in_dim(y, 1 - bit, axis=pos, keepdims=False)
            rounded = lax.reduce_precision(other, exponent_bits=8, mantissa_bits=7)
            high = rounded.astype(jnp.bfloat16)
            low = (other - rounded).astype(jnp.bfloat16)
            message = jnp.concatenate(
                [x.reshape(-1, lanes), high.reshape(-1, lanes), low.reshape(-1, lanes)], axis=0
            )
            perm = [(i, i ^ (1 << j)) for i in range(size)]
            got = lax.ppermute(message, name, perm)
            kept, part = x.size // lanes, high.size // lanes
            x = jnp.concatenate([x, got[:kept].reshape(x.shape)], axis=0)
            y = (
                mine
                + got[kept : kept + part].reshape(high.shape).astype(jnp.float32)
                + got[kept + part :].reshape(high.shape).astype(jnp.float32)
            )
            labels.pop(pos)
    return x, y


def silu_slope(pre):
    sig = jax.nn.sigmoid(pre)
    return sig * (1.0 + pre * (1.0 - sig))


def block(volumes, cotangent, first_weight, second_weight):
    chans = volumes.shape[2]
    half_c = chans // lax.axis_size("ch")
    pair_index = lax.axis_index("ch")
    half_o = first_weight.shape[1]
    sample = lax.all_to_all(volumes, "space", split_axis=1, concat_axis=3, tiled=True)
    depth = sample.shape[3]
    sample = sample.reshape(chans, depth, XY * XY)
    half_z, half_s = (depth // 2, XY // 2)
    voxels = half_z * half_s * half_s
    cols = to_depth(sample, XY)
    pre = lax.dot_general(
        first_weight, cols, (((0,), (0,)), ((), ())), preferred_element_type=jnp.float32
    )
    hidden = jax.nn.silu(pre).astype(jnp.bfloat16)
    grid = lax.all_gather(hidden.reshape(half_o, half_z, half_s, half_s), "ch", axis=0, tiled=True)
    width = grid.shape[0]
    out = conv_forward(grid, second_weight)
    block_out = out.astype(jnp.bfloat16).reshape(1, 1, half_o, half_z, half_s * half_s)
    cot = cotangent.reshape(half_o, voxels)
    factor = 1.0 / math.sqrt(lax.axis_size("space") * lax.axis_size("sub") * voxels)
    cot_grid = cot.reshape(half_o, half_z, half_s, half_s)
    local_rows = second_weight.reshape(27, width, half_o)
    hidden_grad = halving_scatter(conv_back(cot_grid, local_rows), ("ch",))
    pre_grad = (hidden_grad * silu_slope(pre)).astype(jnp.bfloat16)
    grad_first = (
        lax.dot_general(
            cols, pre_grad, (((1,), (1,)), ((), ())), preferred_element_type=jnp.float32
        )
        * factor
    )
    shards = lax.axis_size("space") * lax.axis_size("sub")
    gather_second = shards * (width + half_o) * voxels * 2 <= 1 << 22
    gather_second = gather_second and (grad_first.size // shards) % voxels == 0
    if gather_second:
        both, first_grad = fused_chain(
            jnp.concatenate([grid.reshape(width, voxels), cot], axis=0),
            grad_first,
            ("space", "sub"),
        )
        second_grad = (
            second_grad_rows(
                both[:, :width].reshape(both.shape[0], width, half_z, half_s, half_s),
                both[:, width:],
                ("space", "sub"),
                second_weight.shape[0],
            )
            * factor
        )
    else:
        grad_second = conv_weight_grad(grid, cot) * factor
        first_grad = halving_scatter(grad_first, ("space", "sub"))
        second_grad = halving_scatter(grad_second, ("space", "sub"))
    all_pre_grad = lax.all_gather(pre_grad, "ch", axis=0, tiled=True)
    all_first = lax.all_gather(first_weight, "ch", axis=1, tiled=True)
    first_rows = lax.dynamic_slice_in_dim(
        all_first.reshape(8, chans, width), pair_index * half_c, half_c, 1
    )
    grad_cols = jnp.dot(
        first_rows.reshape(8 * half_c, width), all_pre_grad, preferred_element_type=jnp.float32
    )
    grad_sample = from_depth(grad_cols, half_c, depth, XY).astype(jnp.bfloat16)
    volume_grad = lax.all_to_all(
        grad_sample.reshape(1, 1, half_c, depth, XY * XY),
        "space",
        split_axis=3,
        concat_axis=1,
        tiled=True,
    )
    return (block_out, volume_grad, first_grad, second_grad)


def solution(mesh):
    return step_of(mesh)


def step_of(mesh):
    return jax.shard_map(
        block,
        mesh=mesh,
        in_specs=(
            P(("groups", "sub"), None, None, "space", None),
            P(("groups", "sub"), "space", "ch", None, None),
            P(None, "ch"),
            P(None, "ch"),
        ),
        out_specs=(
            P(("groups", "sub"), "space", "ch", None, None),
            P(("groups", "sub"), None, "ch", "space", None),
            P(("space", "sub"), ("groups", "ch")),
            P(("space", "sub"), ("groups", "ch")),
        ),
        check_vma=False,
    )
```

```python
import math

import jax
import jax.numpy as jnp
from jax import lax
from jax.sharding import PartitionSpec as P


XY = 16


def to_depth(sample, side):
    chans, depth = (sample.shape[0], sample.shape[1])
    blocks = sample.reshape(chans, depth // 2, 2, side // 2, 2, side // 2, 2)
    blocks = blocks.transpose(2, 4, 6, 0, 1, 3, 5)
    return blocks.reshape(8 * chans, depth // 2 * (side // 2) * (side // 2))


def from_depth(cols, chans, depth, side):
    blocks = cols.reshape(2, 2, 2, chans, depth // 2, side // 2, side // 2)
    blocks = blocks.transpose(3, 4, 0, 5, 1, 6, 2)
    return blocks.reshape(chans, depth, side * side)


def plane_stack(padded, plane, depth, side, flip):
    chans = padded.shape[0]
    windows = []
    for inner in range(9):
        b, c = (inner // 3, inner % 3)
        if flip:
            window = padded[
                :, 2 - plane : 2 - plane + depth, 2 - b : 2 - b + side, 2 - c : 2 - c + side
            ]
        else:
            window = padded[:, plane : plane + depth, b : b + side, c : c + side]
        windows.append(window.reshape(chans, depth * side * side))
    return jnp.concatenate(windows, axis=0)


def conv_forward(hidden, weight):
    chans, depth, side = (hidden.shape[0], hidden.shape[1], hidden.shape[2])
    padded = jnp.pad(hidden, ((0, 0), (1, 1), (1, 1), (1, 1)))
    total = jnp.zeros((weight.shape[1], depth * side * side), jnp.float32)
    for plane in range(3):
        stacked = plane_stack(padded, plane, depth, side, False)
        piece = weight[plane * 9 * chans : (plane + 1) * 9 * chans]
        total = total + lax.dot_general(
            piece, stacked, (((0,), (0,)), ((), ())), preferred_element_type=jnp.float32
        )
    return total


def conv_weight_grad(hidden, cot):
    depth, side = (hidden.shape[1], hidden.shape[2])
    padded = jnp.pad(hidden, ((0, 0), (1, 1), (1, 1), (1, 1)))
    pieces = []
    for plane in range(3):
        stacked = plane_stack(padded, plane, depth, side, False)
        pieces.append(
            lax.dot_general(
                stacked, cot, (((1,), (1,)), ((), ())), preferred_element_type=jnp.float32
            )
        )
    return jnp.concatenate(pieces, axis=0)


def conv_back(cot, weight_rows):
    depth, side = (cot.shape[1], cot.shape[2])
    padded = jnp.pad(cot, ((0, 0), (1, 1), (1, 1), (1, 1)))
    total = jnp.zeros((weight_rows.shape[1], depth * side * side), jnp.float32)
    for plane in range(3):
        stacked = plane_stack(padded, plane, depth, side, True)
        group = weight_rows[plane * 9 : (plane + 1) * 9]
        lhs = group.transpose(1, 0, 2).reshape(group.shape[1], 9 * group.shape[2])
        total = total + jnp.dot(lhs, stacked, preferred_element_type=jnp.float32)
    return total


def halving_scatter(x, names):
    sizes = [lax.axis_size(n) for n in names]
    labels = []
    for name, size in zip(names, sizes):
        bits = size.bit_length() - 1
        labels += [(name, j) for j in reversed(range(bits))]
    rows = x.shape[0] // math.prod(sizes)
    x = x.reshape((2,) * len(labels) + (rows,) + x.shape[1:])
    for name, size in reversed(list(zip(names, sizes))):
        for j in range(size.bit_length() - 1):
            pos = labels.index((name, j))
            bit = (lax.axis_index(name) >> j) & 1
            mine = lax.dynamic_index_in_dim(x, bit, axis=pos, keepdims=False)
            other = lax.dynamic_index_in_dim(x, 1 - bit, axis=pos, keepdims=False)
            perm = [(i, i ^ (1 << j)) for i in range(size)]
            x = mine + lax.ppermute(other, name, perm)
            labels.pop(pos)
    return x


def second_grad_rows(hidden_all, cot_all, names, total_rows):
    count, chans, depth, side = hidden_all.shape[0], hidden_all.shape[1], hidden_all.shape[2], hidden_all.shape[3]
    shards = math.prod(lax.axis_size(n) for n in names)
    rows = total_rows // shards
    index = 0
    for name in names:
        index = index * lax.axis_size(name) + lax.axis_index(name)
    first = index * rows
    tap0 = first // chans
    taps = min(27, (rows + 2 * chans - 2) // chans)
    padded = jnp.pad(hidden_all, ((0, 0), (0, 0), (1, 1), (1, 1), (1, 1)))
    pieces = []
    for slot in range(taps):
        tap = jnp.minimum(tap0 + slot, 26)
        window = lax.dynamic_slice(
            padded, (0, 0, tap // 9, (tap // 3) % 3, tap % 3), (count, chans, depth, side, side)
        ).reshape(count, chans, depth * side * side)
        pieces.append(
            lax.dot_general(
                window, cot_all, (((0, 2), (0, 2)), ((), ())), preferred_element_type=jnp.float32
            )
        )
    stacked = jnp.concatenate(pieces, axis=0)
    return lax.dynamic_slice_in_dim(stacked, first - tap0 * chans, rows, 0)


def fused_chain(x, y, names):
    sizes = [lax.axis_size(n) for n in names]
    labels = []
    for name, size in zip(names, sizes):
        labels += [(name, j) for j in reversed(range(size.bit_length() - 1))]
    rows = y.shape[0] // math.prod(sizes)
    y = y.reshape((2,) * len(labels) + (rows,) + y.shape[1:])
    lanes = x.shape[-1]
    x = x[None]
    for name, size in zip(names, sizes):
        for j in reversed(range(size.bit_length() - 1)):
            pos = labels.index((name, j))
            bit = (lax.axis_index(name) >> j) & 1
            mine = lax.dynamic_index_in_dim(y, bit, axis=pos, keepdims=False)
            other = lax.dynamic_index_in_dim(y, 1 - bit, axis=pos, keepdims=False)
            rounded = lax.reduce_precision(other, exponent_bits=8, mantissa_bits=7)
            high = rounded.astype(jnp.bfloat16)
            low = (other - rounded).astype(jnp.bfloat16)
            message = jnp.concatenate(
                [x.reshape(-1, lanes), high.reshape(-1, lanes), low.reshape(-1, lanes)], axis=0
            )
            perm = [(i, i ^ (1 << j)) for i in range(size)]
            got = lax.ppermute(message, name, perm)
            kept, part = x.size // lanes, high.size // lanes
            x = jnp.concatenate([x, got[:kept].reshape(x.shape)], axis=0)
            y = (
                mine
                + got[kept : kept + part].reshape(high.shape).astype(jnp.float32)
                + got[kept + part :].reshape(high.shape).astype(jnp.float32)
            )
            labels.pop(pos)
    return x, y


def regroup(volumes, name):
    size = lax.axis_size(name)
    bits = size.bit_length() - 1
    index = lax.axis_index(name)
    per, chans, planes, area = volumes.shape[1:]
    x = volumes.reshape((2,) * bits + (per // size, chans, planes, area))
    for j in reversed(range(bits)):
        bit = (index >> j) & 1
        mine = lax.dynamic_index_in_dim(x, bit, axis=0, keepdims=False)
        other = lax.dynamic_index_in_dim(x, 1 - bit, axis=0, keepdims=False)
        got = lax.ppermute(other, name, [(i, i ^ (1 << j)) for i in range(size)])
        axis = mine.ndim - 2
        x = jnp.where(bit == 0, jnp.stack([mine, got], axis), jnp.stack([got, mine], axis))
    return x.reshape(per // size, chans, size * planes, area)


def silu_slope(pre):
    sig = jax.nn.sigmoid(pre)
    return sig * (1.0 + pre * (1.0 - sig))


def block(volumes, cotangent, first_weight, second_weight):
    chans = volumes.shape[2]
    half_c = chans // lax.axis_size("ch")
    pair_index = lax.axis_index("ch")
    half_o = first_weight.shape[1]
    sample = regroup(volumes, "space")
    depth = sample.shape[2]
    sample = sample.reshape(chans, depth, XY * XY)
    half_z, half_s = (depth // 2, XY // 2)
    voxels = half_z * half_s * half_s
    cols = to_depth(sample, XY)
    pre = lax.dot_general(
        first_weight, cols, (((0,), (0,)), ((), ())), preferred_element_type=jnp.float32
    )
    hidden = jax.nn.silu(pre).astype(jnp.bfloat16)
    grid = lax.all_gather(hidden.reshape(half_o, half_z, half_s, half_s), "ch", axis=0, tiled=True)
    width = grid.shape[0]
    out = conv_forward(grid, second_weight)
    block_out = out.astype(jnp.bfloat16).reshape(1, 1, half_o, half_z, half_s * half_s)
    cot = cotangent.reshape(half_o, voxels)
    factor = 1.0 / math.sqrt(lax.axis_size("space") * lax.axis_size("sub") * voxels)
    cot_grid = cot.reshape(half_o, half_z, half_s, half_s)
    local_rows = second_weight.reshape(27, width, half_o)
    hidden_grad = halving_scatter(conv_back(cot_grid, local_rows), ("ch",))
    pre_grad = (hidden_grad * silu_slope(pre)).astype(jnp.bfloat16)
    grad_first = (
        lax.dot_general(
            cols, pre_grad, (((1,), (1,)), ((), ())), preferred_element_type=jnp.float32
        )
        * factor
    )
    shards = lax.axis_size("space") * lax.axis_size("sub")
    gather_second = shards * (width + half_o) * voxels * 2 <= 1 << 22
    gather_second = gather_second and (grad_first.size // shards) % voxels == 0
    if gather_second:
        both, first_grad = fused_chain(
            jnp.concatenate([grid.reshape(width, voxels), cot], axis=0),
            grad_first,
            ("space", "sub"),
        )
        second_grad = (
            second_grad_rows(
                both[:, :width].reshape(both.shape[0], width, half_z, half_s, half_s),
                both[:, width:],
                ("space", "sub"),
                second_weight.shape[0],
            )
            * factor
        )
    else:
        grad_second = conv_weight_grad(grid, cot) * factor
        first_grad = halving_scatter(grad_first, ("space", "sub"))
        second_grad = halving_scatter(grad_second, ("space", "sub"))
    all_pre_grad = lax.all_gather(pre_grad, "ch", axis=0, tiled=True)
    all_first = lax.all_gather(first_weight, "ch", axis=1, tiled=True)
    first_rows = lax.dynamic_slice_in_dim(
        all_first.reshape(8, chans, width), pair_index * half_c, half_c, 1
    )
    grad_cols = jnp.dot(
        first_rows.reshape(8 * half_c, width), all_pre_grad, preferred_element_type=jnp.float32
    )
    grad_sample = from_depth(grad_cols, half_c, depth, XY).astype(jnp.bfloat16)
    volume_grad = lax.all_to_all(
        grad_sample.reshape(1, 1, half_c, depth, XY * XY),
        "space",
        split_axis=3,
        concat_axis=1,
        tiled=True,
    )
    return (block_out, volume_grad, first_grad, second_grad)


def solution(mesh):
    return step_of(mesh)


def step_of(mesh):
    return jax.shard_map(
        block,
        mesh=mesh,
        in_specs=(
            P(("groups", "sub"), None, None, "space", None),
            P(("groups", "sub"), "space", "ch", None, None),
            P(None, "ch"),
            P(None, "ch"),
        ),
        out_specs=(
            P(("groups", "sub"), "space", "ch", None, None),
            P(("groups", "sub"), None, "ch", "space", None),
            P(("space", "sub"), ("groups", "ch")),
            P(("space", "sub"), ("groups", "ch")),
        ),
        check_vma=False,
    )
```

```python
import math

import jax
import jax.numpy as jnp
from jax import lax
from jax.sharding import PartitionSpec as P


XY = 16


def to_depth(sample, side):
    chans, depth = (sample.shape[0], sample.shape[1])
    blocks = sample.reshape(chans, depth // 2, 2, side // 2, 2, side // 2, 2)
    blocks = blocks.transpose(2, 4, 6, 0, 1, 3, 5)
    return blocks.reshape(8 * chans, depth // 2 * (side // 2) * (side // 2))


def from_depth(cols, chans, depth, side):
    blocks = cols.reshape(2, 2, 2, chans, depth // 2, side // 2, side // 2)
    blocks = blocks.transpose(3, 4, 0, 5, 1, 6, 2)
    return blocks.reshape(chans, depth, side * side)


def plane_stack(padded, plane, depth, side, flip):
    chans = padded.shape[0]
    windows = []
    for inner in range(9):
        b, c = (inner // 3, inner % 3)
        if flip:
            window = padded[
                :, 2 - plane : 2 - plane + depth, 2 - b : 2 - b + side, 2 - c : 2 - c + side
            ]
        else:
            window = padded[:, plane : plane + depth, b : b + side, c : c + side]
        windows.append(window.reshape(chans, depth * side * side))
    return jnp.concatenate(windows, axis=0)


def conv_forward(hidden, weight):
    chans, depth, side = (hidden.shape[0], hidden.shape[1], hidden.shape[2])
    padded = jnp.pad(hidden, ((0, 0), (1, 1), (1, 1), (1, 1)))
    total = jnp.zeros((weight.shape[1], depth * side * side), jnp.float32)
    for plane in range(3):
        stacked = plane_stack(padded, plane, depth, side, False)
        piece = weight[plane * 9 * chans : (plane + 1) * 9 * chans]
        total = total + lax.dot_general(
            piece, stacked, (((0,), (0,)), ((), ())), preferred_element_type=jnp.float32
        )
    return total


def conv_weight_grad(hidden, cot):
    depth, side = (hidden.shape[1], hidden.shape[2])
    padded = jnp.pad(hidden, ((0, 0), (1, 1), (1, 1), (1, 1)))
    pieces = []
    for plane in range(3):
        stacked = plane_stack(padded, plane, depth, side, False)
        pieces.append(
            lax.dot_general(
                stacked, cot, (((1,), (1,)), ((), ())), preferred_element_type=jnp.float32
            )
        )
    return jnp.concatenate(pieces, axis=0)


def conv_back(cot, weight_rows):
    depth, side = (cot.shape[1], cot.shape[2])
    padded = jnp.pad(cot, ((0, 0), (1, 1), (1, 1), (1, 1)))
    total = jnp.zeros((weight_rows.shape[1], depth * side * side), jnp.float32)
    for plane in range(3):
        stacked = plane_stack(padded, plane, depth, side, True)
        group = weight_rows[plane * 9 : (plane + 1) * 9]
        lhs = group.transpose(1, 0, 2).reshape(group.shape[1], 9 * group.shape[2])
        total = total + jnp.dot(lhs, stacked, preferred_element_type=jnp.float32)
    return total


def halving_scatter(x, names):
    sizes = [lax.axis_size(n) for n in names]
    labels = []
    for name, size in zip(names, sizes):
        bits = size.bit_length() - 1
        labels += [(name, j) for j in reversed(range(bits))]
    rows = x.shape[0] // math.prod(sizes)
    x = x.reshape((2,) * len(labels) + (rows,) + x.shape[1:])
    for name, size in reversed(list(zip(names, sizes))):
        for j in range(size.bit_length() - 1):
            pos = labels.index((name, j))
            bit = (lax.axis_index(name) >> j) & 1
            mine = lax.dynamic_index_in_dim(x, bit, axis=pos, keepdims=False)
            other = lax.dynamic_index_in_dim(x, 1 - bit, axis=pos, keepdims=False)
            perm = [(i, i ^ (1 << j)) for i in range(size)]
            x = mine + lax.ppermute(other, name, perm)
            labels.pop(pos)
    return x


def second_grad_rows(hidden_all, cot_all, names, total_rows):
    count, chans, depth, side = hidden_all.shape[0], hidden_all.shape[1], hidden_all.shape[2], hidden_all.shape[3]
    shards = math.prod(lax.axis_size(n) for n in names)
    rows = total_rows // shards
    index = 0
    for name in names:
        index = index * lax.axis_size(name) + lax.axis_index(name)
    first = index * rows
    tap0 = first // chans
    taps = min(27, (rows + 2 * chans - 2) // chans)
    padded = jnp.pad(hidden_all, ((0, 0), (0, 0), (1, 1), (1, 1), (1, 1)))
    pieces = []
    for slot in range(taps):
        tap = jnp.minimum(tap0 + slot, 26)
        window = lax.dynamic_slice(
            padded, (0, 0, tap // 9, (tap // 3) % 3, tap % 3), (count, chans, depth, side, side)
        ).reshape(count, chans, depth * side * side)
        pieces.append(
            lax.dot_general(
                window, cot_all, (((0, 2), (0, 2)), ((), ())), preferred_element_type=jnp.float32
            )
        )
    stacked = jnp.concatenate(pieces, axis=0)
    return lax.dynamic_slice_in_dim(stacked, first - tap0 * chans, rows, 0)


def fused_chain(x, y, names):
    sizes = [lax.axis_size(n) for n in names]
    labels = []
    for name, size in zip(names, sizes):
        labels += [(name, j) for j in reversed(range(size.bit_length() - 1))]
    rows = y.shape[0] // math.prod(sizes)
    y = y.reshape((2,) * len(labels) + (rows,) + y.shape[1:])
    lanes = x.shape[-1]
    x = x[None]
    for name, size in zip(names, sizes):
        for j in reversed(range(size.bit_length() - 1)):
            pos = labels.index((name, j))
            bit = (lax.axis_index(name) >> j) & 1
            mine = lax.dynamic_index_in_dim(y, bit, axis=pos, keepdims=False)
            other = lax.dynamic_index_in_dim(y, 1 - bit, axis=pos, keepdims=False)
            rounded = lax.reduce_precision(other, exponent_bits=8, mantissa_bits=7)
            high = rounded.astype(jnp.bfloat16)
            low = (other - rounded).astype(jnp.bfloat16)
            message = jnp.concatenate(
                [x.reshape(-1, lanes), high.reshape(-1, lanes), low.reshape(-1, lanes)], axis=0
            )
            perm = [(i, i ^ (1 << j)) for i in range(size)]
            got = lax.ppermute(message, name, perm)
            kept, part = x.size // lanes, high.size // lanes
            x = jnp.concatenate([x, got[:kept].reshape(x.shape)], axis=0)
            y = (
                mine
                + got[kept : kept + part].reshape(high.shape).astype(jnp.float32)
                + got[kept + part :].reshape(high.shape).astype(jnp.float32)
            )
            labels.pop(pos)
    return x, y


def silu_slope(pre):
    sig = jax.nn.sigmoid(pre)
    return sig * (1.0 + pre * (1.0 - sig))


def block(volumes, cotangent, first_weight, second_weight):
    chans = volumes.shape[2]
    half_c = chans // lax.axis_size("ch")
    pair_index = lax.axis_index("ch")
    half_o = first_weight.shape[1]
    sample = lax.all_to_all(volumes, "space", split_axis=1, concat_axis=3, tiled=True)
    depth = sample.shape[3]
    sample = sample.reshape(chans, depth, XY * XY)
    half_z, half_s = (depth // 2, XY // 2)
    voxels = half_z * half_s * half_s
    cols = to_depth(sample, XY)
    all_first = lax.all_gather(first_weight, "ch", axis=1, tiled=True)
    width = all_first.shape[1]
    pre_all = lax.dot_general(
        all_first, cols, (((0,), (0,)), ((), ())), preferred_element_type=jnp.float32
    )
    grid = jax.nn.silu(pre_all).astype(jnp.bfloat16).reshape(width, half_z, half_s, half_s)
    pre = lax.dynamic_slice_in_dim(pre_all, pair_index * half_o, half_o, 0)
    out = conv_forward(grid, second_weight)
    block_out = out.astype(jnp.bfloat16).reshape(1, 1, half_o, half_z, half_s * half_s)
    cot = cotangent.reshape(half_o, voxels)
    factor = 1.0 / math.sqrt(lax.axis_size("space") * lax.axis_size("sub") * voxels)
    cot_grid = cot.reshape(half_o, half_z, half_s, half_s)
    local_rows = second_weight.reshape(27, width, half_o)
    hidden_grad = halving_scatter(conv_back(cot_grid, local_rows), ("ch",))
    pre_grad = (hidden_grad * silu_slope(pre)).astype(jnp.bfloat16)
    grad_first = (
        lax.dot_general(
            cols, pre_grad, (((1,), (1,)), ((), ())), preferred_element_type=jnp.float32
        )
        * factor
    )
    shards = lax.axis_size("space") * lax.axis_size("sub")
    gather_second = shards * (width + half_o) * voxels * 2 <= 1 << 22
    gather_second = gather_second and (grad_first.size // shards) % voxels == 0
    if gather_second:
        both, first_grad = fused_chain(
            jnp.concatenate([grid.reshape(width, voxels), cot], axis=0),
            grad_first,
            ("space", "sub"),
        )
        second_grad = (
            second_grad_rows(
                both[:, :width].reshape(both.shape[0], width, half_z, half_s, half_s),
                both[:, width:],
                ("space", "sub"),
                second_weight.shape[0],
            )
            * factor
        )
    else:
        grad_second = conv_weight_grad(grid, cot) * factor
        first_grad = halving_scatter(grad_first, ("space", "sub"))
        second_grad = halving_scatter(grad_second, ("space", "sub"))
    all_pre_grad = lax.all_gather(pre_grad, "ch", axis=0, tiled=True)
    first_rows = lax.dynamic_slice_in_dim(
        all_first.reshape(8, chans, width), pair_index * half_c, half_c, 1
    )
    grad_cols = jnp.dot(
        first_rows.reshape(8 * half_c, width), all_pre_grad, preferred_element_type=jnp.float32
    )
    grad_sample = from_depth(grad_cols, half_c, depth, XY).astype(jnp.bfloat16)
    volume_grad = lax.all_to_all(
        grad_sample.reshape(1, 1, half_c, depth, XY * XY),
        "space",
        split_axis=3,
        concat_axis=1,
        tiled=True,
    )
    return (block_out, volume_grad, first_grad, second_grad)


def solution(mesh):
    return step_of(mesh)


def step_of(mesh):
    return jax.shard_map(
        block,
        mesh=mesh,
        in_specs=(
            P(("groups", "sub"), None, None, "space", None),
            P(("groups", "sub"), "space", "ch", None, None),
            P(None, "ch"),
            P(None, "ch"),
        ),
        out_specs=(
            P(("groups", "sub"), "space", "ch", None, None),
            P(("groups", "sub"), None, "ch", "space", None),
            P(("space", "sub"), ("groups", "ch")),
            P(("space", "sub"), ("groups", "ch")),
        ),
        check_vma=False,
    )
```

```python
import math

import jax
import jax.numpy as jnp
from jax import lax
from jax.sharding import PartitionSpec as P


XY = 16


def to_depth(sample, side):
    chans, depth = (sample.shape[0], sample.shape[1])
    blocks = sample.reshape(chans, depth // 2, 2, side // 2, 2, side // 2, 2)
    blocks = blocks.transpose(2, 4, 6, 0, 1, 3, 5)
    return blocks.reshape(8 * chans, depth // 2 * (side // 2) * (side // 2))


def from_depth(cols, chans, depth, side):
    blocks = cols.reshape(2, 2, 2, chans, depth // 2, side // 2, side // 2)
    blocks = blocks.transpose(3, 4, 0, 5, 1, 6, 2)
    return blocks.reshape(chans, depth, side * side)


def plane_stack(padded, plane, depth, side, flip):
    chans = padded.shape[0]
    windows = []
    for inner in range(9):
        b, c = (inner // 3, inner % 3)
        if flip:
            window = padded[
                :, 2 - plane : 2 - plane + depth, 2 - b : 2 - b + side, 2 - c : 2 - c + side
            ]
        else:
            window = padded[:, plane : plane + depth, b : b + side, c : c + side]
        windows.append(window.reshape(chans, depth * side * side))
    return jnp.concatenate(windows, axis=0)


def conv_forward(hidden, weight):
    chans, depth, side = (hidden.shape[0], hidden.shape[1], hidden.shape[2])
    padded = jnp.pad(hidden, ((0, 0), (1, 1), (1, 1), (1, 1)))
    total = jnp.zeros((weight.shape[1], depth * side * side), jnp.float32)
    for plane in range(3):
        stacked = plane_stack(padded, plane, depth, side, False)
        piece = weight[plane * 9 * chans : (plane + 1) * 9 * chans]
        total = total + lax.dot_general(
            piece, stacked, (((0,), (0,)), ((), ())), preferred_element_type=jnp.float32
        )
    return total


def conv_weight_grad(hidden, cot):
    depth, side = (hidden.shape[1], hidden.shape[2])
    padded = jnp.pad(hidden, ((0, 0), (1, 1), (1, 1), (1, 1)))
    pieces = []
    for plane in range(3):
        stacked = plane_stack(padded, plane, depth, side, False)
        pieces.append(
            lax.dot_general(
                stacked, cot, (((1,), (1,)), ((), ())), preferred_element_type=jnp.float32
            )
        )
    return jnp.concatenate(pieces, axis=0)


def conv_back(cot, weight_rows):
    depth, side = (cot.shape[1], cot.shape[2])
    padded = jnp.pad(cot, ((0, 0), (1, 1), (1, 1), (1, 1)))
    total = jnp.zeros((weight_rows.shape[1], depth * side * side), jnp.float32)
    for plane in range(3):
        stacked = plane_stack(padded, plane, depth, side, True)
        group = weight_rows[plane * 9 : (plane + 1) * 9]
        lhs = group.transpose(1, 0, 2).reshape(group.shape[1], 9 * group.shape[2])
        total = total + jnp.dot(lhs, stacked, preferred_element_type=jnp.float32)
    return total


def halving_scatter(x, names):
    sizes = [lax.axis_size(n) for n in names]
    labels = []
    for name, size in zip(names, sizes):
        bits = size.bit_length() - 1
        labels += [(name, j) for j in reversed(range(bits))]
    rows = x.shape[0] // math.prod(sizes)
    x = x.reshape((2,) * len(labels) + (rows,) + x.shape[1:])
    for name, size in reversed(list(zip(names, sizes))):
        for j in range(size.bit_length() - 1):
            pos = labels.index((name, j))
            bit = (lax.axis_index(name) >> j) & 1
            mine = lax.dynamic_index_in_dim(x, bit, axis=pos, keepdims=False)
            other = lax.dynamic_index_in_dim(x, 1 - bit, axis=pos, keepdims=False)
            perm = [(i, i ^ (1 << j)) for i in range(size)]
            x = mine + lax.ppermute(other, name, perm)
            labels.pop(pos)
    return x


def second_grad_rows(hidden_all, cot_all, names, total_rows, fence=False):
    count, chans, depth, side = hidden_all.shape[0], hidden_all.shape[1], hidden_all.shape[2], hidden_all.shape[3]
    shards = math.prod(lax.axis_size(n) for n in names)
    rows = total_rows // shards
    index = 0
    for name in names:
        index = index * lax.axis_size(name) + lax.axis_index(name)
    first = index * rows
    if fence:
        first, hidden_all = lax.optimization_barrier((first, hidden_all))
    tap0 = first // chans
    taps = min(27, (rows + 2 * chans - 2) // chans)
    padded = jnp.pad(hidden_all, ((0, 0), (0, 0), (1, 1), (1, 1), (1, 1)))
    pieces = []
    for slot in range(taps):
        tap = jnp.minimum(tap0 + slot, 26)
        window = lax.dynamic_slice(
            padded, (0, 0, tap // 9, (tap // 3) % 3, tap % 3), (count, chans, depth, side, side)
        ).reshape(count, chans, depth * side * side)
        pieces.append(
            lax.dot_general(
                window, cot_all, (((0, 2), (0, 2)), ((), ())), preferred_element_type=jnp.float32
            )
        )
    stacked = jnp.concatenate(pieces, axis=0)
    return lax.dynamic_slice_in_dim(stacked, first - tap0 * chans, rows, 0)


def fused_chain(x, y, names):
    sizes = [lax.axis_size(n) for n in names]
    labels = []
    for name, size in zip(names, sizes):
        labels += [(name, j) for j in reversed(range(size.bit_length() - 1))]
    rows = y.shape[0] // math.prod(sizes)
    y = y.reshape((2,) * len(labels) + (rows,) + y.shape[1:])
    lanes = x.shape[-1]
    x = x[None]
    for name, size in zip(names, sizes):
        for j in reversed(range(size.bit_length() - 1)):
            pos = labels.index((name, j))
            bit = (lax.axis_index(name) >> j) & 1
            mine = lax.dynamic_index_in_dim(y, bit, axis=pos, keepdims=False)
            other = lax.dynamic_index_in_dim(y, 1 - bit, axis=pos, keepdims=False)
            rounded = lax.reduce_precision(other, exponent_bits=8, mantissa_bits=7)
            high = rounded.astype(jnp.bfloat16)
            low = (other - rounded).astype(jnp.bfloat16)
            message = jnp.concatenate(
                [x.reshape(-1, lanes), high.reshape(-1, lanes), low.reshape(-1, lanes)], axis=0
            )
            perm = [(i, i ^ (1 << j)) for i in range(size)]
            got = lax.ppermute(message, name, perm)
            kept, part = x.size // lanes, high.size // lanes
            pieces = (x, got[:kept].reshape(x.shape))
            x = jnp.concatenate(pieces, axis=0)
            y = (
                mine
                + got[kept : kept + part].reshape(high.shape).astype(jnp.float32)
                + got[kept + part :].reshape(high.shape).astype(jnp.float32)
            )
            labels.pop(pos)
    return pieces, y


def silu_slope(pre):
    sig = jax.nn.sigmoid(pre)
    return sig * (1.0 + pre * (1.0 - sig))


def block(volumes, cotangent, first_weight, second_weight):
    chans = volumes.shape[2]
    half_c = chans // lax.axis_size("ch")
    pair_index = lax.axis_index("ch")
    half_o = first_weight.shape[1]
    sample = lax.all_to_all(volumes, "space", split_axis=1, concat_axis=3, tiled=True)
    depth = sample.shape[3]
    sample = sample.reshape(chans, depth, XY * XY)
    half_z, half_s = (depth // 2, XY // 2)
    voxels = half_z * half_s * half_s
    cols = to_depth(sample, XY)
    all_first = lax.all_gather(first_weight, "ch", axis=1, tiled=True)
    width = all_first.shape[1]
    pre_all = lax.dot_general(
        all_first, cols, (((0,), (0,)), ((), ())), preferred_element_type=jnp.float32
    )
    grid = jax.nn.silu(pre_all).astype(jnp.bfloat16).reshape(width, half_z, half_s, half_s)
    pre = lax.dynamic_slice_in_dim(pre_all, pair_index * half_o, half_o, 0)
    out = conv_forward(grid, second_weight)
    block_out = out.astype(jnp.bfloat16).reshape(1, 1, half_o, half_z, half_s * half_s)
    cot = cotangent.reshape(half_o, voxels)
    factor = 1.0 / math.sqrt(lax.axis_size("space") * lax.axis_size("sub") * voxels)
    cot_grid = cot.reshape(half_o, half_z, half_s, half_s)
    local_rows = second_weight.reshape(27, width, half_o)
    hidden_grad = halving_scatter(conv_back(cot_grid, local_rows), ("ch",))
    pre_grad = (hidden_grad * silu_slope(pre)).astype(jnp.bfloat16)
    grad_first = (
        lax.dot_general(
            cols, pre_grad, (((1,), (1,)), ((), ())), preferred_element_type=jnp.float32
        )
        * factor
    )
    shards = lax.axis_size("space") * lax.axis_size("sub")
    gather_second = shards * (width + half_o) * voxels * 2 <= 1 << 22
    gather_second = gather_second and (grad_first.size // shards) % voxels == 0
    if gather_second:
        pieces, first_grad = fused_chain(
            jnp.concatenate([grid.reshape(width, voxels), cot], axis=0),
            grad_first,
            ("space", "sub"),
        )
        half = pieces[0].shape[0]
        terms = []
        for k, part in enumerate(pieces):
            terms.append(second_grad_rows(
                part[:, :width].reshape(half, width, half_z, half_s, half_s),
                part[:, width:],
                ("space", "sub"),
                second_weight.shape[0],
                fence=k == 0,
            ))
        second_grad = (lax.optimization_barrier(terms[0]) + terms[1]) * factor
    else:
        grad_second = conv_weight_grad(grid, cot) * factor
        first_grad = halving_scatter(grad_first, ("space", "sub"))
        second_grad = halving_scatter(grad_second, ("space", "sub"))
    all_pre_grad = lax.all_gather(pre_grad, "ch", axis=0, tiled=True)
    first_rows = lax.dynamic_slice_in_dim(
        all_first.reshape(8, chans, width), pair_index * half_c, half_c, 1
    )
    grad_cols = jnp.dot(
        first_rows.reshape(8 * half_c, width), all_pre_grad, preferred_element_type=jnp.float32
    )
    grad_sample = from_depth(grad_cols, half_c, depth, XY).astype(jnp.bfloat16)
    volume_grad = lax.all_to_all(
        grad_sample.reshape(1, 1, half_c, depth, XY * XY),
        "space",
        split_axis=3,
        concat_axis=1,
        tiled=True,
    )
    return (block_out, volume_grad, first_grad, second_grad)


def solution(mesh):
    return step_of(mesh)


def step_of(mesh):
    return jax.shard_map(
        block,
        mesh=mesh,
        in_specs=(
            P(("groups", "sub"), None, None, "space", None),
            P(("groups", "sub"), "space", "ch", None, None),
            P(None, "ch"),
            P(None, "ch"),
        ),
        out_specs=(
            P(("groups", "sub"), "space", "ch", None, None),
            P(("groups", "sub"), None, "ch", "space", None),
            P(("space", "sub"), ("groups", "ch")),
            P(("space", "sub"), ("groups", "ch")),
        ),
        check_vma=False,
    )
```

```python
import math

import jax
import jax.numpy as jnp
from jax import lax
from jax.sharding import PartitionSpec as P


XY = 16


def to_depth(sample, side):
    chans, depth = (sample.shape[0], sample.shape[1])
    blocks = sample.reshape(chans, depth // 2, 2, side // 2, 2, side // 2, 2)
    blocks = blocks.transpose(2, 4, 6, 0, 1, 3, 5)
    return blocks.reshape(8 * chans, depth // 2 * (side // 2) * (side // 2))


def from_depth(cols, chans, depth, side):
    blocks = cols.reshape(2, 2, 2, chans, depth // 2, side // 2, side // 2)
    blocks = blocks.transpose(3, 4, 0, 5, 1, 6, 2)
    return blocks.reshape(chans, depth, side * side)


def plane_stack(padded, plane, depth, side, flip):
    chans = padded.shape[0]
    windows = []
    for inner in range(9):
        b, c = (inner // 3, inner % 3)
        if flip:
            window = padded[
                :, 2 - plane : 2 - plane + depth, 2 - b : 2 - b + side, 2 - c : 2 - c + side
            ]
        else:
            window = padded[:, plane : plane + depth, b : b + side, c : c + side]
        windows.append(window.reshape(chans, depth * side * side))
    return jnp.concatenate(windows, axis=0)


def conv_forward(hidden, weight):
    chans, depth, side = (hidden.shape[0], hidden.shape[1], hidden.shape[2])
    padded = jnp.pad(hidden, ((0, 0), (1, 1), (1, 1), (1, 1)))
    total = jnp.zeros((weight.shape[1], depth * side * side), jnp.float32)
    for plane in range(3):
        stacked = plane_stack(padded, plane, depth, side, False)
        piece = weight[plane * 9 * chans : (plane + 1) * 9 * chans]
        total = total + lax.dot_general(
            piece, stacked, (((0,), (0,)), ((), ())), preferred_element_type=jnp.float32
        )
    return total


def conv_weight_grad(hidden, cot):
    depth, side = (hidden.shape[1], hidden.shape[2])
    padded = jnp.pad(hidden, ((0, 0), (1, 1), (1, 1), (1, 1)))
    pieces = []
    for plane in range(3):
        stacked = plane_stack(padded, plane, depth, side, False)
        pieces.append(
            lax.dot_general(
                stacked, cot, (((1,), (1,)), ((), ())), preferred_element_type=jnp.float32
            )
        )
    return jnp.concatenate(pieces, axis=0)


def conv_back(cot, weight_rows):
    depth, side = (cot.shape[1], cot.shape[2])
    padded = jnp.pad(cot, ((0, 0), (1, 1), (1, 1), (1, 1)))
    total = jnp.zeros((weight_rows.shape[1], depth * side * side), jnp.float32)
    for plane in range(3):
        stacked = plane_stack(padded, plane, depth, side, True)
        group = weight_rows[plane * 9 : (plane + 1) * 9]
        lhs = group.transpose(1, 0, 2).reshape(group.shape[1], 9 * group.shape[2])
        total = total + jnp.dot(lhs, stacked, preferred_element_type=jnp.float32)
    return total


def halving_scatter(x, names):
    sizes = [lax.axis_size(n) for n in names]
    labels = []
    for name, size in zip(names, sizes):
        bits = size.bit_length() - 1
        labels += [(name, j) for j in reversed(range(bits))]
    rows = x.shape[0] // math.prod(sizes)
    x = x.reshape((2,) * len(labels) + (rows,) + x.shape[1:])
    for name, size in reversed(list(zip(names, sizes))):
        for j in range(size.bit_length() - 1):
            pos = labels.index((name, j))
            bit = (lax.axis_index(name) >> j) & 1
            mine = lax.dynamic_index_in_dim(x, bit, axis=pos, keepdims=False)
            other = lax.dynamic_index_in_dim(x, 1 - bit, axis=pos, keepdims=False)
            perm = [(i, i ^ (1 << j)) for i in range(size)]
            x = mine + lax.ppermute(other, name, perm)
            labels.pop(pos)
    return x


def second_grad_rows(hidden_all, cot_all, names, total_rows):
    count, chans, depth, side = hidden_all.shape[0], hidden_all.shape[1], hidden_all.shape[2], hidden_all.shape[3]
    shards = math.prod(lax.axis_size(n) for n in names)
    rows = total_rows // shards
    index = 0
    for name in names:
        index = index * lax.axis_size(name) + lax.axis_index(name)
    first = index * rows
    tap0 = first // chans
    taps = min(27, (rows + 2 * chans - 2) // chans)
    padded = jnp.pad(hidden_all, ((0, 0), (0, 0), (1, 1), (1, 1), (1, 1)))
    pieces = []
    for slot in range(taps):
        tap = jnp.minimum(tap0 + slot, 26)
        window = lax.dynamic_slice(
            padded, (0, 0, tap // 9, (tap // 3) % 3, tap % 3), (count, chans, depth, side, side)
        ).reshape(count, chans, depth * side * side)
        pieces.append(
            lax.dot_general(
                window, cot_all, (((0, 2), (0, 2)), ((), ())), preferred_element_type=jnp.float32
            )
        )
    stacked = jnp.concatenate(pieces, axis=0)
    return lax.dynamic_slice_in_dim(stacked, first - tap0 * chans, rows, 0)


def fused_chain(x, y, names):
    sizes = [lax.axis_size(n) for n in names]
    labels = []
    for name, size in zip(names, sizes):
        labels += [(name, j) for j in reversed(range(size.bit_length() - 1))]
    rows = y.shape[0] // math.prod(sizes)
    y = y.reshape((2,) * len(labels) + (rows,) + y.shape[1:])
    lanes = x.shape[-1]
    x = x[None]
    for name, size in zip(names, sizes):
        for j in reversed(range(size.bit_length() - 1)):
            pos = labels.index((name, j))
            bit = (lax.axis_index(name) >> j) & 1
            mine = lax.dynamic_index_in_dim(y, bit, axis=pos, keepdims=False)
            other = lax.dynamic_index_in_dim(y, 1 - bit, axis=pos, keepdims=False)
            rounded = lax.reduce_precision(other, exponent_bits=8, mantissa_bits=7)
            high = rounded.astype(jnp.bfloat16)
            low = (other - rounded).astype(jnp.bfloat16)
            message = jnp.concatenate(
                [x.reshape(-1, lanes), high.reshape(-1, lanes), low.reshape(-1, lanes)], axis=0
            )
            perm = [(i, i ^ (1 << j)) for i in range(size)]
            got = lax.ppermute(message, name, perm)
            kept, part = x.size // lanes, high.size // lanes
            x = jnp.concatenate([x, got[:kept].reshape(x.shape)], axis=0)
            y = (
                mine
                + got[kept : kept + part].reshape(high.shape).astype(jnp.float32)
                + got[kept + part :].reshape(high.shape).astype(jnp.float32)
            )
            labels.pop(pos)
    return x, y


def regroup_back(x, name):
    size = lax.axis_size(name)
    bits = size.bit_length() - 1
    index = lax.axis_index(name)
    count, chans, depth, area = x.shape
    x = x.reshape((count, chans) + (2,) * bits + (depth // size, area))
    for j in range(bits):
        bit = (index >> j) & 1
        mine = lax.dynamic_index_in_dim(x, bit, axis=x.ndim - 3, keepdims=False)
        other = lax.dynamic_index_in_dim(x, 1 - bit, axis=x.ndim - 3, keepdims=False)
        got = lax.ppermute(other, name, [(i, i ^ (1 << j)) for i in range(size)])
        x = jnp.where(bit == 0, jnp.stack([mine, got], 0), jnp.stack([got, mine], 0))
    return x.reshape((count * size, chans, depth // size, area))


def silu_slope(pre):
    sig = jax.nn.sigmoid(pre)
    return sig * (1.0 + pre * (1.0 - sig))


def block(volumes, cotangent, first_weight, second_weight):
    chans = volumes.shape[2]
    half_c = chans // lax.axis_size("ch")
    pair_index = lax.axis_index("ch")
    half_o = first_weight.shape[1]
    sample = lax.all_to_all(volumes, "space", split_axis=1, concat_axis=3, tiled=True)
    depth = sample.shape[3]
    sample = sample.reshape(chans, depth, XY * XY)
    half_z, half_s = (depth // 2, XY // 2)
    voxels = half_z * half_s * half_s
    cols = to_depth(sample, XY)
    all_first = lax.all_gather(first_weight, "ch", axis=1, tiled=True)
    width = all_first.shape[1]
    pre_all = lax.dot_general(
        all_first, cols, (((0,), (0,)), ((), ())), preferred_element_type=jnp.float32
    )
    grid = jax.nn.silu(pre_all).astype(jnp.bfloat16).reshape(width, half_z, half_s, half_s)
    pre = lax.dynamic_slice_in_dim(pre_all, pair_index * half_o, half_o, 0)
    out = conv_forward(grid, second_weight)
    block_out = out.astype(jnp.bfloat16).reshape(1, 1, half_o, half_z, half_s * half_s)
    cot = cotangent.reshape(half_o, voxels)
    factor = 1.0 / math.sqrt(lax.axis_size("space") * lax.axis_size("sub") * voxels)
    cot_grid = cot.reshape(half_o, half_z, half_s, half_s)
    local_rows = second_weight.reshape(27, width, half_o)
    hidden_grad = halving_scatter(conv_back(cot_grid, local_rows), ("ch",))
    pre_grad = (hidden_grad * silu_slope(pre)).astype(jnp.bfloat16)
    grad_first = (
        lax.dot_general(
            cols, pre_grad, (((1,), (1,)), ((), ())), preferred_element_type=jnp.float32
        )
        * factor
    )
    shards = lax.axis_size("space") * lax.axis_size("sub")
    gather_second = shards * (width + half_o) * voxels * 2 <= 1 << 22
    gather_second = gather_second and (grad_first.size // shards) % voxels == 0
    if gather_second:
        own_half = lax.dynamic_slice_in_dim(
            grid.reshape(width, voxels), pair_index * half_o, half_o, 0
        )
        both, first_grad = fused_chain(
            jnp.concatenate([own_half, cot], axis=0), grad_first, ("space", "sub")
        )
        mine = both[:, :half_o]
        other = lax.ppermute(mine, "ch", [(0, 1), (1, 0)])
        hidden_all = jnp.where(
            pair_index == 0,
            jnp.concatenate([mine, other], axis=1),
            jnp.concatenate([other, mine], axis=1),
        )
        second_grad = (
            second_grad_rows(
                hidden_all.reshape(both.shape[0], width, half_z, half_s, half_s),
                both[:, half_o:],
                ("space", "sub"),
                second_weight.shape[0],
            )
            * factor
        )
    else:
        grad_second = conv_weight_grad(grid, cot) * factor
        first_grad = halving_scatter(grad_first, ("space", "sub"))
        second_grad = halving_scatter(grad_second, ("space", "sub"))
    all_pre_grad = lax.all_gather(pre_grad, "ch", axis=0, tiled=True)
    first_rows = lax.dynamic_slice_in_dim(
        all_first.reshape(8, chans, width), pair_index * half_c, half_c, 1
    )
    grad_cols = jnp.dot(
        first_rows.reshape(8 * half_c, width), all_pre_grad, preferred_element_type=jnp.float32
    )
    grad_sample = from_depth(grad_cols, half_c, depth, XY).astype(jnp.bfloat16)
    volume_grad = regroup_back(grad_sample.reshape(1, half_c, depth, XY * XY), "space")[None]
    return (block_out, volume_grad, first_grad, second_grad)


def solution(mesh):
    return step_of(mesh)


def step_of(mesh):
    return jax.shard_map(
        block,
        mesh=mesh,
        in_specs=(
            P(("groups", "sub"), None, None, "space", None),
            P(("groups", "sub"), "space", "ch", None, None),
            P(None, "ch"),
            P(None, "ch"),
        ),
        out_specs=(
            P(("groups", "sub"), "space", "ch", None, None),
            P(("groups", "sub"), None, "ch", "space", None),
            P(("space", "sub"), ("groups", "ch")),
            P(("space", "sub"), ("groups", "ch")),
        ),
        check_vma=False,
    )
```

```python
import math

import jax
import jax.numpy as jnp
from jax import lax
from jax.sharding import PartitionSpec as P


XY = 16


def to_depth(sample, side):
    chans, depth = (sample.shape[0], sample.shape[1])
    blocks = sample.reshape(chans, depth // 2, 2, side // 2, 2, side // 2, 2)
    blocks = blocks.transpose(2, 4, 6, 0, 1, 3, 5)
    return blocks.reshape(8 * chans, depth // 2 * (side // 2) * (side // 2))


def from_depth(cols, chans, depth, side):
    blocks = cols.reshape(2, 2, 2, chans, depth // 2, side // 2, side // 2)
    blocks = blocks.transpose(3, 4, 0, 5, 1, 6, 2)
    return blocks.reshape(chans, depth, side * side)


def plane_stack(padded, plane, depth, side, flip):
    chans = padded.shape[0]
    windows = []
    for inner in range(9):
        b, c = (inner // 3, inner % 3)
        if flip:
            window = padded[
                :, 2 - plane : 2 - plane + depth, 2 - b : 2 - b + side, 2 - c : 2 - c + side
            ]
        else:
            window = padded[:, plane : plane + depth, b : b + side, c : c + side]
        windows.append(window.reshape(chans, depth * side * side))
    return jnp.concatenate(windows, axis=0)


def conv_forward(hidden, weight):
    chans, depth, side = (hidden.shape[0], hidden.shape[1], hidden.shape[2])
    padded = jnp.pad(hidden, ((0, 0), (1, 1), (1, 1), (1, 1)))
    total = jnp.zeros((weight.shape[1], depth * side * side), jnp.float32)
    for plane in range(3):
        stacked = plane_stack(padded, plane, depth, side, False)
        piece = weight[plane * 9 * chans : (plane + 1) * 9 * chans]
        total = total + lax.dot_general(
            piece, stacked, (((0,), (0,)), ((), ())), preferred_element_type=jnp.float32
        )
    return total


def conv_weight_grad(hidden, cot):
    depth, side = (hidden.shape[1], hidden.shape[2])
    padded = jnp.pad(hidden, ((0, 0), (1, 1), (1, 1), (1, 1)))
    pieces = []
    for plane in range(3):
        stacked = plane_stack(padded, plane, depth, side, False)
        pieces.append(
            lax.dot_general(
                stacked, cot, (((1,), (1,)), ((), ())), preferred_element_type=jnp.float32
            )
        )
    return jnp.concatenate(pieces, axis=0)


def conv_back(cot, weight_rows):
    depth, side = (cot.shape[1], cot.shape[2])
    padded = jnp.pad(cot, ((0, 0), (1, 1), (1, 1), (1, 1)))
    total = jnp.zeros((weight_rows.shape[1], depth * side * side), jnp.float32)
    for plane in range(3):
        stacked = plane_stack(padded, plane, depth, side, True)
        group = weight_rows[plane * 9 : (plane + 1) * 9]
        lhs = group.transpose(1, 0, 2).reshape(group.shape[1], 9 * group.shape[2])
        total = total + jnp.dot(lhs, stacked, preferred_element_type=jnp.float32)
    return total


def halving_scatter(x, names):
    sizes = [lax.axis_size(n) for n in names]
    labels = []
    for name, size in zip(names, sizes):
        bits = size.bit_length() - 1
        labels += [(name, j) for j in reversed(range(bits))]
    rows = x.shape[0] // math.prod(sizes)
    x = x.reshape((2,) * len(labels) + (rows,) + x.shape[1:])
    for name, size in reversed(list(zip(names, sizes))):
        for j in range(size.bit_length() - 1):
            pos = labels.index((name, j))
            bit = (lax.axis_index(name) >> j) & 1
            mine = lax.dynamic_index_in_dim(x, bit, axis=pos, keepdims=False)
            other = lax.dynamic_index_in_dim(x, 1 - bit, axis=pos, keepdims=False)
            perm = [(i, i ^ (1 << j)) for i in range(size)]
            x = mine + lax.ppermute(other, name, perm)
            labels.pop(pos)
    return x


def second_grad_rows(hidden_all, cot_all, names, total_rows, fence=False):
    count, chans, depth, side = hidden_all.shape[0], hidden_all.shape[1], hidden_all.shape[2], hidden_all.shape[3]
    shards = math.prod(lax.axis_size(n) for n in names)
    rows = total_rows // shards
    index = 0
    for name in names:
        index = index * lax.axis_size(name) + lax.axis_index(name)
    first = index * rows
    if fence:
        first, hidden_all = lax.optimization_barrier((first, hidden_all))
    tap0 = first // chans
    taps = min(27, (rows + 2 * chans - 2) // chans)
    padded = jnp.pad(hidden_all, ((0, 0), (0, 0), (1, 1), (1, 1), (1, 1)))
    pieces = []
    for slot in range(taps):
        tap = jnp.minimum(tap0 + slot, 26)
        window = lax.dynamic_slice(
            padded, (0, 0, tap // 9, (tap // 3) % 3, tap % 3), (count, chans, depth, side, side)
        ).reshape(count, chans, depth * side * side)
        pieces.append(
            lax.dot_general(
                window, cot_all, (((0, 2), (0, 2)), ((), ())), preferred_element_type=jnp.float32
            )
        )
    stacked = jnp.concatenate(pieces, axis=0)
    return lax.dynamic_slice_in_dim(stacked, first - tap0 * chans, rows, 0)


def fused_chain(x, y, names):
    sizes = [lax.axis_size(n) for n in names]
    labels = []
    for name, size in zip(names, sizes):
        labels += [(name, j) for j in reversed(range(size.bit_length() - 1))]
    rows = y.shape[0] // math.prod(sizes)
    y = y.reshape((2,) * len(labels) + (rows,) + y.shape[1:])
    lanes = x.shape[-1]
    x = x[None]
    for name, size in zip(names, sizes):
        for j in reversed(range(size.bit_length() - 1)):
            pos = labels.index((name, j))
            bit = (lax.axis_index(name) >> j) & 1
            mine = lax.dynamic_index_in_dim(y, bit, axis=pos, keepdims=False)
            other = lax.dynamic_index_in_dim(y, 1 - bit, axis=pos, keepdims=False)
            rounded = lax.reduce_precision(other, exponent_bits=8, mantissa_bits=7)
            high = rounded.astype(jnp.bfloat16)
            low = (other - rounded).astype(jnp.bfloat16)
            message = jnp.concatenate(
                [x.reshape(-1, lanes), high.reshape(-1, lanes), low.reshape(-1, lanes)], axis=0
            )
            perm = [(i, i ^ (1 << j)) for i in range(size)]
            got = lax.ppermute(message, name, perm)
            kept, part = x.size // lanes, high.size // lanes
            pieces = (x, got[:kept].reshape(x.shape))
            x = jnp.concatenate(pieces, axis=0)
            y = (
                mine
                + got[kept : kept + part].reshape(high.shape).astype(jnp.float32)
                + got[kept + part :].reshape(high.shape).astype(jnp.float32)
            )
            labels.pop(pos)
    return pieces, y


def silu_slope(pre):
    sig = jax.nn.sigmoid(pre)
    return sig * (1.0 + pre * (1.0 - sig))


def block(volumes, cotangent, first_weight, second_weight):
    chans = volumes.shape[2]
    half_c = chans // lax.axis_size("ch")
    pair_index = lax.axis_index("ch")
    half_o = first_weight.shape[1]
    sample = lax.all_to_all(volumes, "space", split_axis=1, concat_axis=3, tiled=True)
    depth = sample.shape[3]
    sample = sample.reshape(chans, depth, XY * XY)
    half_z, half_s = (depth // 2, XY // 2)
    voxels = half_z * half_s * half_s
    cols = to_depth(sample, XY)
    all_first = lax.all_gather(first_weight, "ch", axis=1, tiled=True)
    width = all_first.shape[1]
    pre_all = lax.dot_general(
        all_first, cols, (((0,), (0,)), ((), ())), preferred_element_type=jnp.float32
    )
    grid = jax.nn.silu(pre_all).astype(jnp.bfloat16).reshape(width, half_z, half_s, half_s)
    pre = lax.dynamic_slice_in_dim(pre_all, pair_index * half_o, half_o, 0)
    out = conv_forward(grid, second_weight)
    block_out = out.astype(jnp.bfloat16).reshape(1, 1, half_o, half_z, half_s * half_s)
    cot = cotangent.reshape(half_o, voxels)
    factor = 1.0 / math.sqrt(lax.axis_size("space") * lax.axis_size("sub") * voxels)
    cot_grid = cot.reshape(half_o, half_z, half_s, half_s)
    local_rows = second_weight.reshape(27, width, half_o)
    hidden_grad = halving_scatter(conv_back(cot_grid, local_rows), ("ch",))
    pre_grad = (hidden_grad * silu_slope(pre)).astype(jnp.bfloat16)
    grad_first = (
        lax.dot_general(
            cols, pre_grad, (((1,), (1,)), ((), ())), preferred_element_type=jnp.float32
        )
        * factor
    )
    shards = lax.axis_size("space") * lax.axis_size("sub")
    gather_second = shards * (width + half_o) * voxels * 2 <= 1 << 22
    gather_second = gather_second and (grad_first.size // shards) % voxels == 0
    if gather_second:
        own_half = lax.dynamic_slice_in_dim(
            grid.reshape(width, voxels), pair_index * half_o, half_o, 0
        )
        pieces, first_grad = fused_chain(
            jnp.concatenate([own_half, cot], axis=0), grad_first, ("space", "sub")
        )
        terms = []
        for k, part in enumerate(pieces):
            mine = part[:, :half_o]
            other = lax.ppermute(mine, "ch", [(0, 1), (1, 0)])
            low = pair_index == 0
            if k == 0:
                low, mine, other = lax.optimization_barrier((low, mine, other))
            hidden_part = jnp.where(
                low,
                jnp.concatenate([mine, other], axis=1),
                jnp.concatenate([other, mine], axis=1),
            )
            terms.append(
                second_grad_rows(
                    hidden_part.reshape(part.shape[0], width, half_z, half_s, half_s),
                    part[:, half_o:],
                    ("space", "sub"),
                    second_weight.shape[0],
                    fence=k == 0,
                )
            )
        second_grad = (lax.optimization_barrier(terms[0]) + terms[1]) * factor
    else:
        grad_second = conv_weight_grad(grid, cot) * factor
        first_grad = halving_scatter(grad_first, ("space", "sub"))
        second_grad = halving_scatter(grad_second, ("space", "sub"))
    all_pre_grad = lax.all_gather(pre_grad, "ch", axis=0, tiled=True)
    first_rows = lax.dynamic_slice_in_dim(
        all_first.reshape(8, chans, width), pair_index * half_c, half_c, 1
    )
    grad_cols = jnp.dot(
        first_rows.reshape(8 * half_c, width), all_pre_grad, preferred_element_type=jnp.float32
    )
    grad_sample = from_depth(grad_cols, half_c, depth, XY).astype(jnp.bfloat16)
    volume_grad = lax.all_to_all(
        grad_sample.reshape(1, 1, half_c, depth, XY * XY),
        "space",
        split_axis=3,
        concat_axis=1,
        tiled=True,
    )
    return (block_out, volume_grad, first_grad, second_grad)


def solution(mesh):
    return step_of(mesh)


def step_of(mesh):
    return jax.shard_map(
        block,
        mesh=mesh,
        in_specs=(
            P(("groups", "sub"), None, None, "space", None),
            P(("groups", "sub"), "space", "ch", None, None),
            P(None, "ch"),
            P(None, "ch"),
        ),
        out_specs=(
            P(("groups", "sub"), "space", "ch", None, None),
            P(("groups", "sub"), None, "ch", "space", None),
            P(("space", "sub"), ("groups", "ch")),
            P(("space", "sub"), ("groups", "ch")),
        ),
        check_vma=False,
    )
```

```python
import math

import jax
import jax.numpy as jnp
from jax import lax
from jax.sharding import PartitionSpec as P


XY = 16


def to_depth(sample, side):
    chans, depth = (sample.shape[0], sample.shape[1])
    blocks = sample.reshape(chans, depth // 2, 2, side // 2, 2, side // 2, 2)
    blocks = blocks.transpose(2, 4, 6, 0, 1, 3, 5)
    return blocks.reshape(8 * chans, depth // 2 * (side // 2) * (side // 2))


def from_depth(cols, chans, depth, side):
    blocks = cols.reshape(2, 2, 2, chans, depth // 2, side // 2, side // 2)
    blocks = blocks.transpose(3, 4, 0, 5, 1, 6, 2)
    return blocks.reshape(chans, depth, side * side)


def plane_stack(padded, plane, depth, side, flip):
    chans = padded.shape[0]
    windows = []
    for inner in range(9):
        b, c = (inner // 3, inner % 3)
        if flip:
            window = padded[
                :, 2 - plane : 2 - plane + depth, 2 - b : 2 - b + side, 2 - c : 2 - c + side
            ]
        else:
            window = padded[:, plane : plane + depth, b : b + side, c : c + side]
        windows.append(window.reshape(chans, depth * side * side))
    return jnp.concatenate(windows, axis=0)


def conv_forward(hidden, weight):
    chans, depth, side = (hidden.shape[0], hidden.shape[1], hidden.shape[2])
    padded = jnp.pad(hidden, ((0, 0), (1, 1), (1, 1), (1, 1)))
    total = jnp.zeros((weight.shape[1], depth * side * side), jnp.float32)
    for plane in range(3):
        stacked = plane_stack(padded, plane, depth, side, False)
        piece = weight[plane * 9 * chans : (plane + 1) * 9 * chans]
        total = total + lax.dot_general(
            piece, stacked, (((0,), (0,)), ((), ())), preferred_element_type=jnp.float32
        )
    return total


def conv_weight_grad(hidden, cot):
    depth, side = (hidden.shape[1], hidden.shape[2])
    padded = jnp.pad(hidden, ((0, 0), (1, 1), (1, 1), (1, 1)))
    pieces = []
    for plane in range(3):
        stacked = plane_stack(padded, plane, depth, side, False)
        pieces.append(
            lax.dot_general(
                stacked, cot, (((1,), (1,)), ((), ())), preferred_element_type=jnp.float32
            )
        )
    return jnp.concatenate(pieces, axis=0)


def conv_back(cot, weight_rows):
    depth, side = (cot.shape[1], cot.shape[2])
    padded = jnp.pad(cot, ((0, 0), (1, 1), (1, 1), (1, 1)))
    total = jnp.zeros((weight_rows.shape[1], depth * side * side), jnp.float32)
    for plane in range(3):
        stacked = plane_stack(padded, plane, depth, side, True)
        group = weight_rows[plane * 9 : (plane + 1) * 9]
        lhs = group.transpose(1, 0, 2).reshape(group.shape[1], 9 * group.shape[2])
        total = total + jnp.dot(lhs, stacked, preferred_element_type=jnp.float32)
    return total


def halving_scatter(x, names):
    sizes = [lax.axis_size(n) for n in names]
    labels = []
    for name, size in zip(names, sizes):
        bits = size.bit_length() - 1
        labels += [(name, j) for j in reversed(range(bits))]
    rows = x.shape[0] // math.prod(sizes)
    x = x.reshape((2,) * len(labels) + (rows,) + x.shape[1:])
    for name, size in reversed(list(zip(names, sizes))):
        for j in range(size.bit_length() - 1):
            pos = labels.index((name, j))
            bit = (lax.axis_index(name) >> j) & 1
            mine = lax.dynamic_index_in_dim(x, bit, axis=pos, keepdims=False)
            other = lax.dynamic_index_in_dim(x, 1 - bit, axis=pos, keepdims=False)
            perm = [(i, i ^ (1 << j)) for i in range(size)]
            x = mine + lax.ppermute(other, name, perm)
            labels.pop(pos)
    return x


def second_grad_rows(hidden_all, cot_all, names, total_rows):
    count, chans, depth, side = hidden_all.shape[0], hidden_all.shape[1], hidden_all.shape[2], hidden_all.shape[3]
    shards = math.prod(lax.axis_size(n) for n in names)
    rows = total_rows // shards
    index = 0
    for name in names:
        index = index * lax.axis_size(name) + lax.axis_index(name)
    first = index * rows
    tap0 = first // chans
    taps = min(27, (rows + 2 * chans - 2) // chans)
    padded = jnp.pad(hidden_all, ((0, 0), (0, 0), (1, 1), (1, 1), (1, 1)))
    pieces = []
    for slot in range(taps):
        tap = jnp.minimum(tap0 + slot, 26)
        window = lax.dynamic_slice(
            padded, (0, 0, tap // 9, (tap // 3) % 3, tap % 3), (count, chans, depth, side, side)
        ).reshape(count, chans, depth * side * side)
        pieces.append(
            lax.dot_general(
                window, cot_all, (((0, 2), (0, 2)), ((), ())), preferred_element_type=jnp.float32
            )
        )
    stacked = jnp.concatenate(pieces, axis=0)
    return lax.dynamic_slice_in_dim(stacked, first - tap0 * chans, rows, 0)


def fused_chain(x, y, names):
    sizes = [lax.axis_size(n) for n in names]
    labels = []
    for name, size in zip(names, sizes):
        labels += [(name, j) for j in reversed(range(size.bit_length() - 1))]
    rows = y.shape[0] // math.prod(sizes)
    y = y.reshape((2,) * len(labels) + (rows,) + y.shape[1:])
    lanes = x.shape[-1]
    x = x[None]
    for name, size in zip(names, sizes):
        for j in reversed(range(size.bit_length() - 1)):
            pos = labels.index((name, j))
            bit = (lax.axis_index(name) >> j) & 1
            mine = lax.dynamic_index_in_dim(y, bit, axis=pos, keepdims=False)
            other = lax.dynamic_index_in_dim(y, 1 - bit, axis=pos, keepdims=False)
            rounded = lax.reduce_precision(other, exponent_bits=8, mantissa_bits=7)
            high = rounded.astype(jnp.bfloat16)
            low = (other - rounded).astype(jnp.bfloat16)
            message = jnp.concatenate(
                [x.reshape(-1, lanes), high.reshape(-1, lanes), low.reshape(-1, lanes)], axis=0
            )
            perm = [(i, i ^ (1 << j)) for i in range(size)]
            got = lax.ppermute(message, name, perm)
            kept, part = x.size // lanes, high.size // lanes
            x = jnp.concatenate([x, got[:kept].reshape(x.shape)], axis=0)
            y = (
                mine
                + got[kept : kept + part].reshape(high.shape).astype(jnp.float32)
                + got[kept + part :].reshape(high.shape).astype(jnp.float32)
            )
            labels.pop(pos)
    return x, y


def silu_slope(pre):
    sig = jax.nn.sigmoid(pre)
    return sig * (1.0 + pre * (1.0 - sig))


def block(volumes, cotangent, first_weight, second_weight):
    chans = volumes.shape[2]
    half_c = chans // lax.axis_size("ch")
    pair_index = lax.axis_index("ch")
    half_o = first_weight.shape[1]
    sample = lax.all_to_all(volumes, "space", split_axis=1, concat_axis=3, tiled=True)
    depth = sample.shape[3]
    sample = sample.reshape(chans, depth, XY * XY)
    half_z, half_s = (depth // 2, XY // 2)
    voxels = half_z * half_s * half_s
    cols = to_depth(sample, XY)
    all_first = lax.all_gather(first_weight, "ch", axis=1, tiled=True)
    width = all_first.shape[1]
    pre_all = lax.dot_general(
        all_first, cols, (((0,), (0,)), ((), ())), preferred_element_type=jnp.float32
    )
    grid = jax.nn.silu(pre_all).astype(jnp.bfloat16).reshape(width, half_z, half_s, half_s)
    pre = lax.dynamic_slice_in_dim(pre_all, pair_index * half_o, half_o, 0)
    out = conv_forward(grid, second_weight)
    block_out = out.astype(jnp.bfloat16).reshape(1, 1, half_o, half_z, half_s * half_s)
    cot = cotangent.reshape(half_o, voxels)
    factor = 1.0 / math.sqrt(lax.axis_size("space") * lax.axis_size("sub") * voxels)
    cot_grid = cot.reshape(half_o, half_z, half_s, half_s)
    local_rows = second_weight.reshape(27, width, half_o)
    hidden_grad = halving_scatter(conv_back(cot_grid, local_rows), ("ch",))
    pre_grad = (hidden_grad * silu_slope(pre)).astype(jnp.bfloat16)
    grad_first = (
        lax.dot_general(
            cols, pre_grad, (((1,), (1,)), ((), ())), preferred_element_type=jnp.float32
        )
        * factor
    )
    shards = lax.axis_size("space") * lax.axis_size("sub")
    gather_second = shards * (width + half_o) * voxels * 2 <= 1 << 22
    gather_second = gather_second and (grad_first.size // shards) % voxels == 0
    if gather_second:
        own_half = lax.dynamic_slice_in_dim(
            grid.reshape(width, voxels), pair_index * half_o, half_o, 0
        )
        both, first_grad = fused_chain(
            jnp.concatenate([own_half, cot], axis=0), grad_first, ("space", "sub")
        )
        mine = both[:, :half_o]
        other = lax.ppermute(mine, "ch", [(0, 1), (1, 0)])
        hidden_all = jnp.where(
            pair_index == 0,
            jnp.concatenate([mine, other], axis=1),
            jnp.concatenate([other, mine], axis=1),
        )
        second_grad = (
            second_grad_rows(
                hidden_all.reshape(both.shape[0], width, half_z, half_s, half_s),
                both[:, half_o:],
                ("space", "sub"),
                second_weight.shape[0],
            )
            * factor
        )
    else:
        grad_second = conv_weight_grad(grid, cot) * factor
        first_grad = halving_scatter(grad_first, ("space", "sub"))
        second_grad = halving_scatter(grad_second, ("space", "sub"))
    all_pre_grad = lax.all_gather(pre_grad, "ch", axis=0, tiled=True)
    first_rows = lax.dynamic_slice_in_dim(
        all_first.reshape(8, chans, width), pair_index * half_c, half_c, 1
    )
    grad_cols = jnp.dot(
        first_rows.reshape(8 * half_c, width), all_pre_grad, preferred_element_type=jnp.float32
    )
    grad_sample = from_depth(grad_cols, half_c, depth, XY).astype(jnp.bfloat16)
    volume_grad = lax.all_to_all(
        grad_sample.reshape(1, 1, half_c, depth, XY * XY),
        "space",
        split_axis=3,
        concat_axis=1,
        tiled=True,
    )
    return (block_out, volume_grad, first_grad, second_grad)


def solution(mesh):
    return step_of(mesh)


def step_of(mesh):
    return jax.shard_map(
        block,
        mesh=mesh,
        in_specs=(
            P(("groups", "sub"), None, None, "space", None),
            P(("groups", "sub"), "space", "ch", None, None),
            P(None, "ch"),
            P(None, "ch"),
        ),
        out_specs=(
            P(("groups", "sub"), "space", "ch", None, None),
            P(("groups", "sub"), None, "ch", "space", None),
            P(("space", "sub"), ("groups", "ch")),
            P(("space", "sub"), ("groups", "ch")),
        ),
        check_vma=False,
    )
```

```python
import math

import jax
import jax.numpy as jnp
from jax import lax
from jax.sharding import PartitionSpec as P


XY = 16


def to_depth(sample, side):
    chans, depth = (sample.shape[0], sample.shape[1])
    blocks = sample.reshape(chans, depth // 2, 2, side // 2, 2, side // 2, 2)
    blocks = blocks.transpose(2, 4, 6, 0, 1, 3, 5)
    return blocks.reshape(8 * chans, depth // 2 * (side // 2) * (side // 2))


def from_depth(cols, chans, depth, side):
    blocks = cols.reshape(2, 2, 2, chans, depth // 2, side // 2, side // 2)
    blocks = blocks.transpose(3, 4, 0, 5, 1, 6, 2)
    return blocks.reshape(chans, depth, side * side)


def plane_stack(padded, plane, depth, side, flip):
    chans = padded.shape[0]
    windows = []
    for inner in range(9):
        b, c = (inner // 3, inner % 3)
        if flip:
            window = padded[
                :, 2 - plane : 2 - plane + depth, 2 - b : 2 - b + side, 2 - c : 2 - c + side
            ]
        else:
            window = padded[:, plane : plane + depth, b : b + side, c : c + side]
        windows.append(window.reshape(chans, depth * side * side))
    return jnp.concatenate(windows, axis=0)


def conv_forward(hidden, weight):
    chans, depth, side = (hidden.shape[0], hidden.shape[1], hidden.shape[2])
    padded = jnp.pad(hidden, ((0, 0), (1, 1), (1, 1), (1, 1)))
    total = jnp.zeros((weight.shape[1], depth * side * side), jnp.float32)
    for plane in range(3):
        stacked = plane_stack(padded, plane, depth, side, False)
        piece = weight[plane * 9 * chans : (plane + 1) * 9 * chans]
        total = total + lax.dot_general(
            piece, stacked, (((0,), (0,)), ((), ())), preferred_element_type=jnp.float32
        )
    return total


def conv_weight_grad(hidden, cot):
    depth, side = (hidden.shape[1], hidden.shape[2])
    padded = jnp.pad(hidden, ((0, 0), (1, 1), (1, 1), (1, 1)))
    pieces = []
    for plane in range(3):
        stacked = plane_stack(padded, plane, depth, side, False)
        pieces.append(
            lax.dot_general(
                stacked, cot, (((1,), (1,)), ((), ())), preferred_element_type=jnp.float32
            )
        )
    return jnp.concatenate(pieces, axis=0)


def conv_back(cot, weight_rows):
    depth, side = (cot.shape[1], cot.shape[2])
    padded = jnp.pad(cot, ((0, 0), (1, 1), (1, 1), (1, 1)))
    total = jnp.zeros((weight_rows.shape[1], depth * side * side), jnp.float32)
    for plane in range(3):
        stacked = plane_stack(padded, plane, depth, side, True)
        group = weight_rows[plane * 9 : (plane + 1) * 9]
        lhs = group.transpose(1, 0, 2).reshape(group.shape[1], 9 * group.shape[2])
        total = total + jnp.dot(lhs, stacked, preferred_element_type=jnp.float32)
    return total


def halving_scatter(x, names):
    sizes = [lax.axis_size(n) for n in names]
    labels = []
    for name, size in zip(names, sizes):
        bits = size.bit_length() - 1
        labels += [(name, j) for j in reversed(range(bits))]
    rows = x.shape[0] // math.prod(sizes)
    x = x.reshape((2,) * len(labels) + (rows,) + x.shape[1:])
    for name, size in reversed(list(zip(names, sizes))):
        for j in range(size.bit_length() - 1):
            pos = labels.index((name, j))
            bit = (lax.axis_index(name) >> j) & 1
            mine = lax.dynamic_index_in_dim(x, bit, axis=pos, keepdims=False)
            other = lax.dynamic_index_in_dim(x, 1 - bit, axis=pos, keepdims=False)
            perm = [(i, i ^ (1 << j)) for i in range(size)]
            x = mine + lax.ppermute(other, name, perm)
            labels.pop(pos)
    return x


def second_grad_rows(hidden_all, cot_all, names, total_rows):
    count, chans, depth, side = hidden_all.shape[0], hidden_all.shape[1], hidden_all.shape[2], hidden_all.shape[3]
    shards = math.prod(lax.axis_size(n) for n in names)
    rows = total_rows // shards
    index = 0
    for name in names:
        index = index * lax.axis_size(name) + lax.axis_index(name)
    first = index * rows
    tap0 = first // chans
    taps = min(27, (rows + 2 * chans - 2) // chans)
    padded = jnp.pad(hidden_all, ((0, 0), (0, 0), (1, 1), (1, 1), (1, 1)))
    pieces = []
    for slot in range(taps):
        tap = jnp.minimum(tap0 + slot, 26)
        window = lax.dynamic_slice(
            padded, (0, 0, tap // 9, (tap // 3) % 3, tap % 3), (count, chans, depth, side, side)
        ).reshape(count, chans, depth * side * side)
        pieces.append(
            lax.dot_general(
                window, cot_all, (((0, 2), (0, 2)), ((), ())), preferred_element_type=jnp.float32
            )
        )
    stacked = jnp.concatenate(pieces, axis=0)
    return lax.dynamic_slice_in_dim(stacked, first - tap0 * chans, rows, 0)


def fused_chain(x, y, names):
    sizes = [lax.axis_size(n) for n in names]
    labels = []
    for name, size in zip(names, sizes):
        labels += [(name, j) for j in reversed(range(size.bit_length() - 1))]
    rows = y.shape[0] // math.prod(sizes)
    y = y.reshape((2,) * len(labels) + (rows,) + y.shape[1:])
    lanes = x.shape[-1]
    x = x[None]
    for name, size in zip(names, sizes):
        for j in reversed(range(size.bit_length() - 1)):
            pos = labels.index((name, j))
            bit = (lax.axis_index(name) >> j) & 1
            mine = lax.dynamic_index_in_dim(y, bit, axis=pos, keepdims=False)
            other = lax.dynamic_index_in_dim(y, 1 - bit, axis=pos, keepdims=False)
            rounded = lax.reduce_precision(other, exponent_bits=8, mantissa_bits=7)
            high = rounded.astype(jnp.bfloat16)
            low = (other - rounded).astype(jnp.bfloat16)
            message = jnp.concatenate(
                [x.reshape(-1, lanes), high.reshape(-1, lanes), low.reshape(-1, lanes)], axis=0
            )
            perm = [(i, i ^ (1 << j)) for i in range(size)]
            got = lax.ppermute(message, name, perm)
            kept, part = x.size // lanes, high.size // lanes
            x = jnp.concatenate([x, got[:kept].reshape(x.shape)], axis=0)
            y = (
                mine
                + got[kept : kept + part].reshape(high.shape).astype(jnp.float32)
                + got[kept + part :].reshape(high.shape).astype(jnp.float32)
            )
            labels.pop(pos)
    return x, y


def silu_slope(pre):
    sig = jax.nn.sigmoid(pre)
    return sig * (1.0 + pre * (1.0 - sig))


def block(volumes, cotangent, first_weight, second_weight):
    chans = volumes.shape[2]
    half_c = chans // lax.axis_size("ch")
    pair_index = lax.axis_index("ch")
    half_o = first_weight.shape[1]
    sample = lax.all_to_all(volumes, "space", split_axis=1, concat_axis=3, tiled=True)
    depth = sample.shape[3]
    sample = sample.reshape(chans, depth, XY * XY)
    half_z, half_s = (depth // 2, XY // 2)
    voxels = half_z * half_s * half_s
    cols = to_depth(sample, XY)
    all_first = lax.all_gather(first_weight, "ch", axis=1, tiled=True)
    width = all_first.shape[1]
    pre_all = lax.dot_general(
        all_first, cols, (((0,), (0,)), ((), ())), preferred_element_type=jnp.float32
    )
    grid = jax.nn.silu(pre_all).astype(jnp.bfloat16).reshape(width, half_z, half_s, half_s)
    pre = lax.dynamic_slice_in_dim(pre_all, pair_index * half_o, half_o, 0)
    out = conv_forward(grid, second_weight)
    block_out = out.astype(jnp.bfloat16).reshape(1, 1, half_o, half_z, half_s * half_s)
    cot = cotangent.reshape(half_o, voxels)
    factor = 1.0 / math.sqrt(lax.axis_size("space") * lax.axis_size("sub") * voxels)
    cot_grid = cot.reshape(half_o, half_z, half_s, half_s)
    local_rows = second_weight.reshape(27, width, half_o)
    hidden_grad = halving_scatter(conv_back(cot_grid, local_rows), ("ch",))
    pre_grad = (hidden_grad * silu_slope(pre)).astype(jnp.bfloat16)
    grad_first = (
        lax.dot_general(
            cols, pre_grad, (((1,), (1,)), ((), ())), preferred_element_type=jnp.float32
        )
        * factor
    )
    shards = lax.axis_size("space") * lax.axis_size("sub")
    gather_second = shards * (width + half_o) * voxels * 2 <= 1 << 22
    gather_second = gather_second and (grad_first.size // shards) % voxels == 0
    if gather_second:
        own_half = lax.dynamic_slice_in_dim(
            grid.reshape(width, voxels), pair_index * half_o, half_o, 0
        )
        both, first_grad = fused_chain(
            jnp.concatenate([own_half, cot], axis=0), grad_first, ("space", "sub")
        )
        mine = both[:, :half_o]
        other = lax.ppermute(mine, "ch", [(0, 1), (1, 0)])
        hidden_all = jnp.where(
            pair_index == 0,
            jnp.concatenate([mine, other], axis=1),
            jnp.concatenate([other, mine], axis=1),
        )
        second_grad = (
            second_grad_rows(
                hidden_all.reshape(both.shape[0], width, half_z, half_s, half_s),
                both[:, half_o:],
                ("space", "sub"),
                second_weight.shape[0],
            )
            * factor
        )
    else:
        grad_second = conv_weight_grad(grid, cot) * factor
        first_grad = halving_scatter(grad_first, ("space", "sub"))
        second_grad = halving_scatter(grad_second, ("space", "sub"))
    if lax.axis_size("ch") == 2:
        other_grad = lax.ppermute(pre_grad, "ch", [(0, 1), (1, 0)])
        all_pre_grad = jnp.where(
            pair_index == 0,
            jnp.concatenate([pre_grad, other_grad], axis=0),
            jnp.concatenate([other_grad, pre_grad], axis=0),
        )
    else:
        all_pre_grad = lax.all_gather(pre_grad, "ch", axis=0, tiled=True)
    first_rows = lax.dynamic_slice_in_dim(
        all_first.reshape(8, chans, width), pair_index * half_c, half_c, 1
    )
    grad_cols = jnp.dot(
        first_rows.reshape(8 * half_c, width), all_pre_grad, preferred_element_type=jnp.float32
    )
    grad_sample = from_depth(grad_cols, half_c, depth, XY).astype(jnp.bfloat16)
    volume_grad = lax.all_to_all(
        grad_sample.reshape(1, 1, half_c, depth, XY * XY),
        "space",
        split_axis=3,
        concat_axis=1,
        tiled=True,
    )
    return (block_out, volume_grad, first_grad, second_grad)


def solution(mesh):
    return step_of(mesh)


def step_of(mesh):
    return jax.shard_map(
        block,
        mesh=mesh,
        in_specs=(
            P(("groups", "sub"), None, None, "space", None),
            P(("groups", "sub"), "space", "ch", None, None),
            P(None, "ch"),
            P(None, "ch"),
        ),
        out_specs=(
            P(("groups", "sub"), "space", "ch", None, None),
            P(("groups", "sub"), None, "ch", "space", None),
            P(("space", "sub"), ("groups", "ch")),
            P(("space", "sub"), ("groups", "ch")),
        ),
        check_vma=False,
    )
```
